256 devices in a mesh: seq: 16 (over z_lo, y), head: 16 (over z_hi, x, core).
Axes of the slice: x: 4, y: 4, z: 8 (z_hi: 2, z_lo: 4; z = z_hi * 4 + z_lo), core: 2. Of those that a mesh axis runs over, the one named last changes fastest.
Arguments:
- queries: bfloat16 [32768, 4096], P(('seq', 'head')), may hold values from -5 to 5
- key_vectors: bfloat16 [32768, 1024], P(('seq', 'head')), may hold values from -5 to 5
- value_vectors: bfloat16 [32768, 1024], P(('seq', 'head')), may hold values from -6 to 6
- doc_lengths: int32 [32], replicated, may hold values from 1 to 4096, 32768 in all
Outputs:
- attended: bfloat16 [32768, 4096], P(('seq', 'head'))
The draws below stay inside these ranges and needn't reach their ends.
Inputs may be any that keep to these rules, and one draw needn't show every extreme that they name: `doc_lengths`: the lengths sum to 32768, and the longest is exactly 4096.
All inputs are finite; a program needn't handle non-finite values.
Results may differ from the reference program's by a relative error of at most 0.0038.
Values may be sent and summed in bfloat16 or wider, within the bound.
No kernel may reach another device: no remote copies, remote signals or barrier semaphores. Data moves between devices by JAX's collectives and lax.ppermute only.
A program may use at most 64 MiB of HBM per device.

```python
import math
import jax
import jax.numpy as jnp
import numpy as np
from jax import lax

QH = 32
KVH = 8
HD = 128
SLOC = 2048
TOKENS = 32768
MAXDOC = 4096
NDOCS = 32


def draw_queries(key, part):
    normal_part = jax.random.normal(jax.random.fold_in(key, 1), (TOKENS, QH * HD), jnp.float32)
    result = jnp.clip(normal_part, -4.5, 4.5)
    return result.astype(jnp.bfloat16)


def draw_key_vectors(key, part):
    normal_part = jax.random.normal(jax.random.fold_in(key, 4), (TOKENS, KVH * HD), jnp.float32)
    result = jnp.clip(normal_part, -4.5, 4.5)
    return result.astype(jnp.bfloat16)


def steps_of(rng, shape, pieces, least, high):
    level, own = 1.0, jax.random.fold_in(rng, 6)
    for position, shards_of in pieces:
        heights = jnp.exp(jax.random.uniform(jax.random.fold_in(own, position), (shards_of,), jnp.float32, least / len(pieces), high / len(pieces)))
        level = level * jnp.repeat(heights, shape[position] // shards_of).reshape([-1 if axis == position else 1 for axis in range(len(shape))])
    return level


def split_up(amount, total, limit, slope):
    weights = [(1 << 20) // math.isqrt(standing ** slope) + 1 for standing in range(2, amount + 1)]
    rest, holding = total - limit - (amount - 1), [1] * (amount - 1)
    while rest > 0:
        candidates = [i for i in range(amount - 1) if holding[i] < limit]
        pool, remaining = sum([weights[i] for i in candidates]), rest
        for i in candidates:
            addition = min(limit - holding[i], max(1, remaining * weights[i] // pool), rest)
            holding[i] = holding[i] + addition
            rest = rest - addition
    return np.array([limit] + holding)


def ragged_sizes(stream_key, amount, total, bound, skew):
    if amount == 2:
        one = jax.random.randint(stream_key, (), max(1, total - bound), min(bound, total - 1) + 1)
        return jnp.stack([one, total - one])
    sizes = jnp.asarray(split_up(amount, total, bound, skew), jnp.int32)
    pairs = (amount - 1) // 2
    source_of, sink = sizes[1:1 + 2 * pairs:2], sizes[2:2 + 2 * pairs:2]
    room = jnp.minimum(source_of - 1, bound - sink)
    passed = jax.random.randint(jax.random.fold_in(stream_key, 1), (pairs,), 0, 1 << 20) % (room + 1)
    sizes = sizes.at[1:1 + 2 * pairs:2].set(source_of - passed).at[2:2 + 2 * pairs:2].set(sink + passed)
    return sizes[jax.random.permutation(jax.random.fold_in(stream_key, 2), amount)]


def gaussian(key, extent, width, most, shards=(), kind=jnp.bfloat16):
    drawn = width * jax.random.normal(key, extent, jnp.float32)
    if shards:
        drawn = drawn * steps_of(key, extent, shards, -0.22, 0.18)
    return jnp.clip(drawn, -most, most).astype(kind)


def setup_inputs(seed: int = 0) -> dict:
    key_list = jax.random.split(jax.random.key(seed), 5)
    return {
        "queries": draw_queries(jax.random.fold_in(key_list[4], 71), 0),
        "key_vectors": draw_key_vectors(jax.random.fold_in(key_list[4], 71), 0),
        "value_vectors": gaussian(key_list[2], (TOKENS, KVH * HD), 1.0, 6.0, ((0, 256),)),
        "doc_lengths": ragged_sizes(key_list[3], NDOCS, TOKENS, MAXDOC, 2).astype(jnp.int32),
    }


def document_ids(doc_lengths, positions):
    doc_ends = jnp.cumsum(doc_lengths).astype(jnp.int32)
    return lax.optimization_barrier(jnp.sum((doc_ends[None, :] <= positions[:, None]).astype(jnp.int32), axis=1))

def reference(queries, key_vectors, value_vectors, doc_lengths):
    block_rows = min(512, SLOC)
    group_size = QH // KVH
    window = MAXDOC + block_rows
    padding = jnp.zeros((MAXDOC, KVH * HD), key_vectors.dtype)
    keys_padded = jnp.concatenate([padding, key_vectors], axis=0)
    values_padded = jnp.concatenate([padding, value_vectors], axis=0)
    scaling = 1.0 / math.sqrt(HD)

    def one_block(offset):
        query_rows = lax.dynamic_slice_in_dim(queries, offset, block_rows, 0).astype(jnp.float32).reshape(block_rows, KVH, group_size, HD)
        key_rows = lax.dynamic_slice_in_dim(keys_padded, offset, window, 0).astype(jnp.float32).reshape(window, KVH, HD)
        value_rows = lax.dynamic_slice_in_dim(values_padded, offset, window, 0).astype(jnp.float32).reshape(window, KVH, HD)
        query_pos = offset + jnp.arange(block_rows, dtype=jnp.int32)
        key_pos = offset - MAXDOC + jnp.arange(window, dtype=jnp.int32)
        allowed = (document_ids(doc_lengths, query_pos)[:, None] == document_ids(doc_lengths, key_pos)[None, :]) & (key_pos[None, :] <= query_pos[:, None]) & (key_pos[None, :] >= 0)
        mask_wide = allowed[:, None, None, :]
        scores = jnp.einsum('qkgd,tkd->qkgt', query_rows, key_rows) * scaling
        masked = jnp.where(mask_wide, scores, -jnp.inf)
        row_max = lax.optimization_barrier(jnp.max(masked, axis=-1, keepdims=True))
        weights_raw = jnp.where(mask_wide, jnp.exp(scores - row_max), 0.0)
        totals = lax.optimization_barrier(jnp.sum(weights_raw, axis=-1))
        rounded = lax.optimization_barrier(weights_raw.astype(jnp.bfloat16)).astype(jnp.float32)
        blended = jnp.einsum('qkgt,tkd->qkgd', rounded, value_rows) / totals[..., None]
        return blended.reshape(block_rows, QH * HD).astype(jnp.bfloat16)
    starts = jnp.arange(TOKENS // block_rows, dtype=jnp.int32) * block_rows
    return lax.map(one_block, starts).reshape(TOKENS, QH * HD)
```

```python
import functools
import math

import jax
import jax.numpy as jnp
from jax import lax
from jax.experimental import pallas as pl
from jax.experimental.pallas import tpu as pltpu
from jax.sharding import PartitionSpec as P

HD = 128
SPAN = 2
BQ = 256
BK = 512


def passed_along(shard, axis, by):
    size = lax.axis_size(axis)
    pairs = [(i, i + by) for i in range(size) if 0 <= i + by < size]
    return lax.ppermute(shard, axis, pairs)


def document_ids(doc_ends, positions):
    return jnp.sum((doc_ends[None, :] <= positions[:, None]).astype(jnp.int32), axis=1)


def document_starts(doc_ends, positions):
    before = doc_ends[None, :] <= positions[:, None]
    return jnp.max(jnp.where(before, doc_ends[None, :], 0), axis=1)


def attention_kernel(lo_ref, hi_ref, q_ref, kv_ref, qd_ref, kd_ref, o_ref, m_sc, l_sc, acc_sc,
                     *, heads, key_offset, scaling):
    block = pl.program_id(0)
    lo = lo_ref[block]
    hi = hi_ref[block]
    q_first = key_offset + block * BQ
    rows = q_first + lax.broadcasted_iota(jnp.int32, (BQ, 1), 0)
    q_docs = qd_ref[...]
    m_sc[...] = jnp.full(m_sc.shape, -1e30, jnp.float32)
    l_sc[...] = jnp.zeros(l_sc.shape, jnp.float32)
    acc_sc[...] = jnp.zeros(acc_sc.shape, jnp.float32)

    def step(j, carry):
        start = pl.multiple_of(j * BK, BK)
        keys = kv_ref[pl.ds(start, BK), 0:HD]
        values = kv_ref[pl.ds(start, BK), HD:2 * HD]
        k_docs = kd_ref[:, pl.ds(start, BK)]
        cols = start + lax.broadcasted_iota(jnp.int32, (1, BK), 1)
        allowed = (q_docs == k_docs) & (cols <= rows)
        for h in range(heads):
            q = q_ref[:, h * HD:(h + 1) * HD]
            s = lax.dot_general(q, keys, (((1,), (1,)), ((), ())),
                                preferred_element_type=jnp.float32) * scaling
            m_prev = m_sc[h]
            m_new = jnp.maximum(m_prev, jnp.max(jnp.where(allowed, s, -1e30), axis=-1, keepdims=True))
            e = jnp.where(allowed, jnp.exp(s - m_new), 0.0)
            fading = jnp.exp(m_prev - m_new)
            l_sc[h] = l_sc[h] * fading + jnp.sum(e, axis=-1, keepdims=True)
            acc_sc[h] = acc_sc[h] * fading + jnp.dot(e.astype(jnp.bfloat16), values,
                                                     preferred_element_type=jnp.float32)
            m_sc[h] = m_new
        return carry

    lax.fori_loop(lo, hi, step, 0)
    for h in range(heads):
        o_ref[:, h * HD:(h + 1) * HD] = (acc_sc[h] / l_sc[h]).astype(o_ref.dtype)


def attend(local_q, kv_all, q_docs, k_docs, lo, hi, heads, key_offset):
    rows = local_q.shape[0]
    keys = kv_all.shape[0]
    kernel = functools.partial(attention_kernel, heads=heads, key_offset=key_offset,
                               scaling=1.0 / math.sqrt(HD))
    grid_spec = pltpu.PrefetchScalarGridSpec(
        num_scalar_prefetch=2,
        grid=(rows // BQ,),
        in_specs=[
            pl.BlockSpec((BQ, heads * HD), lambda i, lo, hi: (i, 0)),
            pl.BlockSpec((keys, 2 * HD), lambda i, lo, hi: (0, 0)),
            pl.BlockSpec((BQ, 1), lambda i, lo, hi: (i, 0)),
            pl.BlockSpec((1, keys), lambda i, lo, hi: (0, 0)),
        ],
        out_specs=pl.BlockSpec((BQ, heads * HD), lambda i, lo, hi: (i, 0)),
        scratch_shapes=[
            pltpu.VMEM((heads, BQ, 1), jnp.float32),
            pltpu.VMEM((heads, BQ, 1), jnp.float32),
            pltpu.VMEM((heads, BQ, HD), jnp.float32),
        ],
    )
    return pl.pallas_call(
        kernel,
        grid_spec=grid_spec,
        out_shape=jax.ShapeDtypeStruct((rows, heads * HD), jnp.bfloat16),
        compiler_params=pltpu.CompilerParams(dimension_semantics=("arbitrary",)),
    )(lo, hi, local_q, kv_all, q_docs.reshape(rows, 1), k_docs.reshape(1, keys))


def on_device(queries, key_vectors, value_vectors, doc_lengths):
    head_dim = HD
    token_rows = queries.shape[0]
    query_total = queries.shape[1] // head_dim
    key_total = key_vectors.shape[1] // head_dim
    devices = lax.axis_size("head")
    heads = query_total // devices
    per_group = devices // key_total
    q_part = queries.reshape(token_rows, devices, heads * head_dim)
    k_part = jnp.repeat(key_vectors.reshape(token_rows, key_total, head_dim), per_group, axis=1)
    v_part = jnp.repeat(value_vectors.reshape(token_rows, key_total, head_dim), per_group, axis=1)
    message = jnp.concatenate([q_part, k_part, v_part], axis=2).reshape(token_rows, -1)
    arrived = lax.all_to_all(message, "head", split_axis=1, concat_axis=0, tiled=True)
    width = heads * head_dim
    local_q = arrived[:, :width]
    paired = arrived[:, width:]
    shard_rows = local_q.shape[0]
    earlier = [passed_along(paired, "seq", distance) for distance in range(SPAN, 0, -1)]
    kv_all = jnp.concatenate(earlier + [paired], axis=0)

    doc_ends = jnp.cumsum(doc_lengths).astype(jnp.int32)
    shard_first = lax.axis_index("seq") * shard_rows
    key_offset = SPAN * shard_rows
    offsets = jnp.arange(shard_rows, dtype=jnp.int32)
    query_pos = shard_first + offsets
    q_docs = document_ids(doc_ends, query_pos)
    key_pos = shard_first - key_offset + jnp.arange(kv_all.shape[0], dtype=jnp.int32)
    k_docs = jnp.where(key_pos >= 0, document_ids(doc_ends, key_pos), -1)
    block_first = query_pos[::BQ]
    starts = document_starts(doc_ends, block_first) - (shard_first - key_offset)
    lo = jnp.maximum(starts, 0) // BK
    hi = (key_offset + jnp.arange(shard_rows // BQ, dtype=jnp.int32) * BQ + BQ - 1) // BK + 1
    blocks = attend(local_q, kv_all, q_docs, k_docs, lo.astype(jnp.int32), hi.astype(jnp.int32),
                    heads, key_offset)
    return lax.all_to_all(blocks, "head", split_axis=0, concat_axis=1, tiled=True)


def solution(mesh):
    return jax.shard_map(
        on_device,
        mesh=mesh,
        in_specs=(
            P(("seq", "head"), None),
            P(("seq", "head"), None),
            P(("seq", "head"), None),
            P(),
        ),
        out_specs=P(("seq", "head"), None),
        check_vma=False,
    )
```

```python
import functools
import math

import jax
import jax.numpy as jnp
from jax import lax
from jax.experimental import pallas as pl
from jax.experimental.pallas import tpu as pltpu
from jax.sharding import Mesh
from jax.sharding import PartitionSpec as P

HD = 128
KVH = 8
MAXDOC = 4096
BQ = 256
BK = 512
TOKEN_AXES = ("seq", "zhi")


def passed_along(shard, axis, by):
    size = lax.axis_size(axis)
    pairs = [(i, i + by) for i in range(size) if 0 <= i + by < size]
    return lax.ppermute(shard, axis, pairs)


def document_ids(doc_ends, positions):
    return jnp.sum((doc_ends[None, :] <= positions[:, None]).astype(jnp.int32), axis=1)


def document_starts(doc_ends, positions):
    before = doc_ends[None, :] <= positions[:, None]
    return jnp.max(jnp.where(before, doc_ends[None, :], 0), axis=1)


def attention_kernel(lo_ref, hi_ref, q_ref, kv_ref, qd_ref, kd_ref, *rest, heads, causal, first,
                     last, scaling):
    if first:
        o_refs, (m_sc, l_sc, acc_sc) = rest[:-3], rest[-3:]
    else:
        (m_in, l_in, acc_in), o_refs, (m_sc, l_sc, acc_sc) = rest[:3], rest[3:-3], rest[-3:]
    block = pl.program_id(0)
    lo = lo_ref[block]
    hi = hi_ref[block]
    rows = block * BQ + lax.broadcasted_iota(jnp.int32, (BQ, 1), 0)
    q_docs = qd_ref[...]
    if first:
        m_sc[...] = jnp.full(m_sc.shape, -1e30, jnp.float32)
        l_sc[...] = jnp.zeros(l_sc.shape, jnp.float32)
        acc_sc[...] = jnp.zeros(acc_sc.shape, jnp.float32)
    else:
        m_sc[...] = m_in[...]
        l_sc[...] = l_in[...]
        acc_sc[...] = acc_in[...]

    def step(j, carry):
        start = pl.multiple_of(j * BK, BK)
        keys = kv_ref[pl.ds(start, BK), 0:HD]
        values = kv_ref[pl.ds(start, BK), HD:2 * HD]
        allowed = q_docs == kd_ref[:, pl.ds(start, BK)]
        if causal:
            cols = start + lax.broadcasted_iota(jnp.int32, (1, BK), 1)
            allowed = allowed & (cols <= rows)
        for h in range(heads):
            q = q_ref[:, h * HD:(h + 1) * HD]
            s = lax.dot_general(q, keys, (((1,), (1,)), ((), ())),
                                preferred_element_type=jnp.float32) * scaling
            m_prev = m_sc[h]
            m_new = jnp.maximum(m_prev, jnp.max(jnp.where(allowed, s, -1e30), axis=-1, keepdims=True))
            e = jnp.where(allowed, jnp.exp(s - m_new), 0.0)
            fading = jnp.exp(m_prev - m_new)
            l_sc[h] = l_sc[h] * fading + jnp.sum(e, axis=-1, keepdims=True)
            acc_sc[h] = acc_sc[h] * fading + jnp.dot(e.astype(jnp.bfloat16), values,
                                                     preferred_element_type=jnp.float32)
            m_sc[h] = m_new
        return carry

    lax.fori_loop(lo, hi, step, 0)
    if last:
        (o_ref,) = o_refs
        for h in range(heads):
            o_ref[:, h * HD:(h + 1) * HD] = (acc_sc[h] / l_sc[h]).astype(o_ref.dtype)
    else:
        m_out, l_out, acc_out = o_refs
        m_out[...] = m_sc[...]
        l_out[...] = l_sc[...]
        acc_out[...] = acc_sc[...]


def attend(local_q, kv, q_docs, k_docs, lo, hi, state, heads, causal, last):
    rows = local_q.shape[0]
    keys = kv.shape[0]
    first = state is None
    kernel = functools.partial(attention_kernel, heads=heads, causal=causal, first=first,
                               last=last, scaling=1.0 / math.sqrt(HD))
    state_specs = [
        pl.BlockSpec((heads, BQ, 1), lambda i, lo, hi: (0, i, 0)),
        pl.BlockSpec((heads, BQ, 1), lambda i, lo, hi: (0, i, 0)),
        pl.BlockSpec((heads, BQ, HD), lambda i, lo, hi: (0, i, 0)),
    ]
    state_shapes = [
        jax.ShapeDtypeStruct((heads, rows, 1), jnp.float32),
        jax.ShapeDtypeStruct((heads, rows, 1), jnp.float32),
        jax.ShapeDtypeStruct((heads, rows, HD), jnp.float32),
    ]
    in_specs = [
        pl.BlockSpec((BQ, heads * HD), lambda i, lo, hi: (i, 0)),
        pl.BlockSpec((keys, 2 * HD), lambda i, lo, hi: (0, 0)),
        pl.BlockSpec((BQ, 1), lambda i, lo, hi: (i, 0)),
        pl.BlockSpec((1, keys), lambda i, lo, hi: (0, 0)),
    ]
    operands = [lo, hi, local_q, kv, q_docs.reshape(rows, 1), k_docs.reshape(1, keys)]
    if not first:
        in_specs += state_specs
        operands += list(state)
    if last:
        out_specs = pl.BlockSpec((BQ, heads * HD), lambda i, lo, hi: (i, 0))
        out_shape = jax.ShapeDtypeStruct((rows, heads * HD), jnp.bfloat16)
    else:
        out_specs = state_specs
        out_shape = state_shapes
    grid_spec = pltpu.PrefetchScalarGridSpec(
        num_scalar_prefetch=2,
        grid=(rows // BQ,),
        in_specs=in_specs,
        out_specs=out_specs,
        scratch_shapes=[
            pltpu.VMEM((heads, BQ, 1), jnp.float32),
            pltpu.VMEM((heads, BQ, 1), jnp.float32),
            pltpu.VMEM((heads, BQ, HD), jnp.float32),
        ],
    )
    return pl.pallas_call(
        kernel,
        grid_spec=grid_spec,
        out_shape=out_shape,
        compiler_params=pltpu.CompilerParams(dimension_semantics=("arbitrary",)),
    )(*operands)


def on_device(queries, key_vectors, value_vectors, doc_lengths):
    head_dim = HD
    token_rows = queries.shape[0]
    query_total = queries.shape[1] // head_dim
    groups = lax.axis_size("hx")
    heads = query_total // groups
    message = jnp.concatenate(
        [
            queries.reshape(token_rows, groups, heads * head_dim),
            key_vectors.reshape(token_rows, groups, head_dim),
            value_vectors.reshape(token_rows, groups, head_dim),
        ],
        axis=2,
    ).reshape(token_rows, -1)
    arrived = lax.all_to_all(message, "hx", split_axis=1, concat_axis=0, tiled=True)
    width = heads * head_dim
    local_q = arrived[:, :width]
    own = arrived[:, width:]
    chunk_rows = local_q.shape[0]
    behind = MAXDOC // chunk_rows
    previous = [passed_along(own, TOKEN_AXES, 1)]
    per_seq = lax.axis_size("zhi")
    for distance in range(2, behind + 1):
        hop, rest = divmod(distance, per_seq)
        source = own if rest == 0 else previous[rest - 1]
        previous.append(passed_along(source, "seq", hop))
    kv_before = jnp.concatenate(previous[::-1], axis=0)

    doc_ends = jnp.cumsum(doc_lengths).astype(jnp.int32)
    chunk = lax.axis_index("seq") * per_seq + lax.axis_index("zhi")
    chunk_first = chunk * chunk_rows
    query_pos = chunk_first + jnp.arange(chunk_rows, dtype=jnp.int32)
    q_docs = document_ids(doc_ends, query_pos)
    before_rows = kv_before.shape[0]
    before_pos = chunk_first - before_rows + jnp.arange(before_rows, dtype=jnp.int32)
    before_docs = jnp.where(before_pos >= 0, document_ids(doc_ends, before_pos), -1)
    block_first = query_pos[::BQ]
    doc_first = document_starts(doc_ends, block_first)
    lo_own = jnp.maximum(doc_first - chunk_first, 0) // BK
    hi_own = (jnp.arange(chunk_rows // BQ, dtype=jnp.int32) * BQ + BQ - 1) // BK + 1
    lo_before = jnp.minimum(jnp.maximum(doc_first - (chunk_first - before_rows), 0) // BK,
                            before_rows // BK)
    hi_before = jnp.full_like(lo_before, before_rows // BK)
    state = attend(local_q, own, q_docs, q_docs, lo_own.astype(jnp.int32), hi_own.astype(jnp.int32),
                   None, heads, True, False)
    blocks = attend(local_q, kv_before, q_docs, before_docs, lo_before.astype(jnp.int32),
                    hi_before.astype(jnp.int32), state, heads, False, True)
    return lax.all_to_all(blocks, "hx", split_axis=0, concat_axis=1, tiled=True)


def solution(mesh):
    seq = mesh.shape["seq"]
    head = mesh.shape["head"]
    split = head // KVH
    token_mesh = Mesh(mesh.devices.reshape(seq, split, head // split), ("seq", "zhi", "hx"))
    rows = P(("seq", "zhi", "hx"), None)
    return jax.shard_map(
        on_device,
        mesh=token_mesh,
        in_specs=(rows, rows, rows, P()),
        out_specs=rows,
        check_vma=False,
    )
```

```python
import functools
import math

import jax
import jax.numpy as jnp
from jax import lax
from jax.experimental import pallas as pl
from jax.experimental.pallas import tpu as pltpu
from jax.sharding import Mesh
from jax.sharding import PartitionSpec as P

HD = 128
KVH = 8
MAXDOC = 4096
BQ = 128
BK = 512
TOKEN_AXES = ("seq", "zhi")


def passed_along(shard, axis, by):
    size = lax.axis_size(axis)
    pairs = [(i, i + by) for i in range(size) if 0 <= i + by < size]
    return lax.ppermute(shard, axis, pairs)


def document_ids(doc_ends, positions):
    return jnp.sum((doc_ends[None, :] <= positions[:, None]).astype(jnp.int32), axis=1)


def document_starts(doc_ends, positions):
    before = doc_ends[None, :] <= positions[:, None]
    return jnp.max(jnp.where(before, doc_ends[None, :], 0), axis=1)


def attention_kernel(lo_ref, hi_ref, qdf_ref, qdl_ref, kdf_ref, kdl_ref, q_ref, kt_ref, v_ref,
                     qd_ref, qp_ref, kd_ref, *rest, heads, causal, first, last, scaling):
    if first:
        o_refs, (m_sc, l_sc, acc_sc) = rest[:-3], rest[-3:]
    else:
        (m_in, l_in, acc_in), o_refs, (m_sc, l_sc, acc_sc) = rest[:3], rest[3:-3], rest[-3:]
    block = pl.program_id(0)
    lo = lo_ref[block]
    hi = hi_ref[block]
    q_doc_first = qdf_ref[block]
    q_single = q_doc_first == qdl_ref[block]
    stacked = heads * BQ
    q = q_ref[...].reshape(stacked, HD)
    q_docs = qd_ref[...].reshape(stacked, 1)
    q_rows = qp_ref[...].reshape(stacked, 1)
    if first:
        m_sc[...] = jnp.full(m_sc.shape, -1e30, jnp.float32)
        l_sc[...] = jnp.zeros(l_sc.shape, jnp.float32)
        acc_sc[...] = jnp.zeros(acc_sc.shape, jnp.float32)
    else:
        m_sc[...] = m_in[...].reshape(stacked, 1)
        l_sc[...] = l_in[...].reshape(stacked, 1)
        acc_sc[...] = acc_in[...].reshape(stacked, HD)

    def update(start, masked):
        keys = kt_ref[:, pl.ds(start, BK)]
        values = v_ref[pl.ds(start, BK), :]
        s = jnp.dot(q, keys, preferred_element_type=jnp.float32) * scaling
        m_prev = m_sc[...]
        if masked:
            allowed = q_docs == kd_ref[:, pl.ds(start, BK)]
            if causal:
                cols = start + lax.broadcasted_iota(jnp.int32, (1, BK), 1)
                allowed = allowed & (cols <= q_rows)
            m_new = jnp.maximum(m_prev, jnp.max(jnp.where(allowed, s, -1e30), axis=-1, keepdims=True))
            e = jnp.where(allowed, jnp.exp(s - m_new), 0.0)
        else:
            m_new = jnp.maximum(m_prev, jnp.max(s, axis=-1, keepdims=True))
            e = jnp.exp(s - m_new)
        fading = jnp.exp(m_prev - m_new)
        l_sc[...] = l_sc[...] * fading + jnp.sum(e, axis=-1, keepdims=True)
        acc_sc[...] = acc_sc[...] * fading + jnp.dot(e.astype(jnp.bfloat16), values,
                                                     preferred_element_type=jnp.float32)
        m_sc[...] = m_new

    def step(j, carry):
        start = pl.multiple_of(j * BK, BK)
        k_doc_first = kdf_ref[j]
        whole = q_single & (k_doc_first == kdl_ref[j]) & (k_doc_first == q_doc_first)
        if causal:
            whole = whole & (start + BK - 1 <= block * BQ)

        @pl.when(whole)
        def _():
            update(start, False)

        @pl.when(jnp.logical_not(whole))
        def _():
            update(start, True)

        return carry

    lax.fori_loop(lo, hi, step, 0)
    if last:
        (o_ref,) = o_refs
        o_ref[...] = (acc_sc[...] / l_sc[...]).reshape(heads, BQ, HD).astype(o_ref.dtype)
    else:
        m_out, l_out, acc_out = o_refs
        m_out[...] = m_sc[...].reshape(heads, BQ, 1)
        l_out[...] = l_sc[...].reshape(heads, BQ, 1)
        acc_out[...] = acc_sc[...].reshape(heads, BQ, HD)


def attend(head_q, keys_t, values, q_docs, k_docs, lo, hi, state, causal, last):
    heads, rows, _ = head_q.shape
    keys = values.shape[0]
    first = state is None
    kernel = functools.partial(attention_kernel, heads=heads, causal=causal, first=first,
                               last=last, scaling=1.0 / math.sqrt(HD))
    per_block = lambda i, *_: (0, i, 0)
    whole = lambda i, *_: (0, 0)
    state_specs = [
        pl.BlockSpec((heads, BQ, 1), per_block),
        pl.BlockSpec((heads, BQ, 1), per_block),
        pl.BlockSpec((heads, BQ, HD), per_block),
    ]
    state_shapes = [
        jax.ShapeDtypeStruct((heads, rows, 1), jnp.float32),
        jax.ShapeDtypeStruct((heads, rows, 1), jnp.float32),
        jax.ShapeDtypeStruct((heads, rows, HD), jnp.float32),
    ]
    in_specs = [
        pl.BlockSpec((heads, BQ, HD), per_block),
        pl.BlockSpec((HD, keys), whole),
        pl.BlockSpec((keys, HD), whole),
        pl.BlockSpec((heads, BQ, 1), per_block),
        pl.BlockSpec((heads, BQ, 1), per_block),
        pl.BlockSpec((1, keys), whole),
    ]
    q_rows = jnp.broadcast_to(jnp.arange(rows, dtype=jnp.int32)[None, :, None], (heads, rows, 1))
    operands = [
        lo, hi, q_docs[::BQ], q_docs[BQ - 1::BQ], k_docs[::BK], k_docs[BK - 1::BK],
        head_q, keys_t, values, jnp.broadcast_to(q_docs[None, :, None], (heads, rows, 1)), q_rows,
        k_docs.reshape(1, keys),
    ]
    if not first:
        in_specs += state_specs
        operands += list(state)
    if last:
        out_specs = pl.BlockSpec((heads, BQ, HD), per_block)
        out_shape = jax.ShapeDtypeStruct((heads, rows, HD), jnp.bfloat16)
    else:
        out_specs = state_specs
        out_shape = state_shapes
    grid_spec = pltpu.PrefetchScalarGridSpec(
        num_scalar_prefetch=6,
        grid=(rows // BQ,),
        in_specs=in_specs,
        out_specs=out_specs,
        scratch_shapes=[
            pltpu.VMEM((heads * BQ, 1), jnp.float32),
            pltpu.VMEM((heads * BQ, 1), jnp.float32),
            pltpu.VMEM((heads * BQ, HD), jnp.float32),
        ],
    )
    return pl.pallas_call(
        kernel,
        grid_spec=grid_spec,
        out_shape=out_shape,
        compiler_params=pltpu.CompilerParams(dimension_semantics=("arbitrary",)),
    )(*operands)


def on_device(queries, key_vectors, value_vectors, doc_lengths):
    head_dim = HD
    token_rows = queries.shape[0]
    query_total = queries.shape[1] // head_dim
    groups = lax.axis_size("hx")
    heads = query_total // groups
    message = jnp.concatenate(
        [
            queries.reshape(token_rows, groups, heads * head_dim),
            key_vectors.reshape(token_rows, groups, head_dim),
            value_vectors.reshape(token_rows, groups, head_dim),
        ],
        axis=2,
    ).reshape(token_rows, -1)
    arrived = lax.all_to_all(message, "hx", split_axis=1, concat_axis=0, tiled=True)
    width = heads * head_dim
    local_q = arrived[:, :width]
    own = arrived[:, width:]
    chunk_rows = local_q.shape[0]
    behind = MAXDOC // chunk_rows
    previous = [passed_along(own, TOKEN_AXES, 1)]
    per_seq = lax.axis_size("zhi")
    for distance in range(2, behind + 1):
        hop, rest = divmod(distance, per_seq)
        source = own if rest == 0 else previous[rest - 1]
        previous.append(passed_along(source, "seq", hop))
    kv_before = jnp.concatenate(previous[::-1], axis=0)

    doc_ends = jnp.cumsum(doc_lengths).astype(jnp.int32)
    chunk = lax.axis_index("seq") * per_seq + lax.axis_index("zhi")
    chunk_first = chunk * chunk_rows
    query_pos = chunk_first + jnp.arange(chunk_rows, dtype=jnp.int32)
    q_docs = document_ids(doc_ends, query_pos)
    before_rows = kv_before.shape[0]
    before_pos = chunk_first - before_rows + jnp.arange(before_rows, dtype=jnp.int32)
    before_docs = jnp.where(before_pos >= 0, document_ids(doc_ends, before_pos), -1)
    block_first = query_pos[::BQ]
    doc_first = document_starts(doc_ends, block_first)
    lo_own = jnp.maximum(doc_first - chunk_first, 0) // BK
    hi_own = (jnp.arange(chunk_rows // BQ, dtype=jnp.int32) * BQ + BQ - 1) // BK + 1
    lo_before = jnp.minimum(jnp.maximum(doc_first - (chunk_first - before_rows), 0) // BK,
                            before_rows // BK)
    hi_before = jnp.full_like(lo_before, before_rows // BK)
    head_q = local_q.reshape(chunk_rows, heads, head_dim).transpose(1, 0, 2)
    state = attend(head_q, own[:, :head_dim].T, own[:, head_dim:], q_docs, q_docs,
                   lo_own.astype(jnp.int32), hi_own.astype(jnp.int32), None, True, False)
    finished = attend(head_q, kv_before[:, :head_dim].T, kv_before[:, head_dim:], q_docs,
                      before_docs, lo_before.astype(jnp.int32), hi_before.astype(jnp.int32), state,
                      False, True)
    blocks = finished.transpose(1, 0, 2).reshape(chunk_rows, heads * head_dim)
    return lax.all_to_all(blocks, "hx", split_axis=0, concat_axis=1, tiled=True)


def solution(mesh):
    seq = mesh.shape["seq"]
    head = mesh.shape["head"]
    split = head // KVH
    token_mesh = Mesh(mesh.devices.reshape(seq, split, head // split), ("seq", "zhi", "hx"))
    rows = P(("seq", "zhi", "hx"), None)
    return jax.shard_map(
        on_device,
        mesh=token_mesh,
        in_specs=(rows, rows, rows, P()),
        out_specs=rows,
        check_vma=False,
    )
```

```python
import functools
import math

import jax
import jax.numpy as jnp
from jax import lax
from jax.experimental import pallas as pl
from jax.experimental.pallas import tpu as pltpu
from jax.sharding import Mesh
from jax.sharding import PartitionSpec as P

HD = 128
KVH = 8
MAXDOC = 4096
BQ = 256
BK = 512
TOKEN_AXES = ("seq", "zhi")


def passed_along(shard, axis, by):
    size = lax.axis_size(axis)
    pairs = [(i, i + by) for i in range(size) if 0 <= i + by < size]
    return lax.ppermute(shard, axis, pairs)


def document_ids(doc_ends, positions):
    return jnp.sum((doc_ends[None, :] <= positions[:, None]).astype(jnp.int32), axis=1)


def document_starts(doc_ends, positions):
    before = doc_ends[None, :] <= positions[:, None]
    return jnp.max(jnp.where(before, doc_ends[None, :], 0), axis=1)


def attention_kernel(lo_ref, hi_ref, qdf_ref, qdl_ref, kdf_ref, kdl_ref, q_ref, kt_ref, v_ref,
                     qd_ref, kd_ref, *rest, heads, causal, first, last, scaling):
    if first:
        o_refs, (m_sc, l_sc, acc_sc) = rest[:-3], rest[-3:]
    else:
        (m_in, l_in, acc_in), o_refs, (m_sc, l_sc, acc_sc) = rest[:3], rest[3:-3], rest[-3:]
    block = pl.program_id(0)
    lo = lo_ref[block]
    hi = hi_ref[block]
    q_doc_first = qdf_ref[block]
    q_single = q_doc_first == qdl_ref[block]
    lanes = acc_sc.shape[-1]
    reps = BK // lanes
    if first:
        m_sc[...] = jnp.full(m_sc.shape, -1e30, jnp.float32)
        l_sc[...] = jnp.zeros(l_sc.shape, jnp.float32)
        acc_sc[...] = jnp.zeros(acc_sc.shape, jnp.float32)
    else:
        m_sc[...] = jnp.broadcast_to(m_in[...], m_sc.shape)
        l_sc[...] = jnp.broadcast_to(l_in[...], l_sc.shape)
        acc_sc[...] = acc_in[...]

    def update(start, masked):
        keys = kt_ref[:, pl.ds(start, BK)]
        values = v_ref[pl.ds(start, BK), :]
        if masked:
            allowed = jnp.tile(qd_ref[...], (1, reps)) == kd_ref[:, pl.ds(start, BK)]
            if causal:
                rows = block * BQ + lax.broadcasted_iota(jnp.int32, (BQ, BK), 0)
                cols = start + lax.broadcasted_iota(jnp.int32, (BQ, BK), 1)
                allowed = allowed & (cols <= rows)
        for h in range(heads):
            q = q_ref[:, h * HD:(h + 1) * HD]
            s = jnp.dot(q, keys, preferred_element_type=jnp.float32) * scaling
            if masked:
                s = jnp.where(allowed, s, -1e30)
            m_prev = m_sc[h]
            m_next = jnp.maximum(m_prev, jnp.max(s, axis=-1, keepdims=True))
            e = jnp.exp(s - jnp.tile(m_next, (1, reps)))
            if masked:
                e = jnp.where(allowed, e, 0.0)
            fading = jnp.exp(m_prev - m_next)
            l_sc[h] = l_sc[h] * fading + jnp.sum(e, axis=-1, keepdims=True)
            acc_sc[h] = acc_sc[h] * fading + jnp.dot(e.astype(jnp.bfloat16), values,
                                                     preferred_element_type=jnp.float32)
            m_sc[h] = m_next

    def step(j, carry):
        start = pl.multiple_of(j * BK, BK)
        k_doc_first = kdf_ref[j]
        whole = q_single & (k_doc_first == kdl_ref[j]) & (k_doc_first == q_doc_first)
        if causal:
            whole = whole & (start + BK - 1 <= block * BQ)

        @pl.when(whole)
        def _():
            update(start, False)

        @pl.when(jnp.logical_not(whole))
        def _():
            update(start, True)

        return carry

    lax.fori_loop(lo, hi, step, 0)
    if last:
        (o_ref,) = o_refs
        for h in range(heads):
            o_ref[:, h * HD:(h + 1) * HD] = (acc_sc[h] / l_sc[h]).astype(o_ref.dtype)
    else:
        m_out, l_out, acc_out = o_refs
        m_out[...] = m_sc[:, :, 0:1]
        l_out[...] = l_sc[:, :, 0:1]
        acc_out[...] = acc_sc[...]


def attend(local_q, keys_t, values, q_docs, k_docs, lo, hi, state, heads, causal, last):
    rows = local_q.shape[0]
    keys = values.shape[0]
    first = state is None
    kernel = functools.partial(attention_kernel, heads=heads, causal=causal, first=first,
                               last=last, scaling=1.0 / math.sqrt(HD))
    per_block = lambda i, *_: (0, i, 0)
    whole = lambda i, *_: (0, 0)
    state_specs = [
        pl.BlockSpec((heads, BQ, 1), per_block),
        pl.BlockSpec((heads, BQ, 1), per_block),
        pl.BlockSpec((heads, BQ, HD), per_block),
    ]
    state_shapes = [
        jax.ShapeDtypeStruct((heads, rows, 1), jnp.float32),
        jax.ShapeDtypeStruct((heads, rows, 1), jnp.float32),
        jax.ShapeDtypeStruct((heads, rows, HD), jnp.float32),
    ]
    in_specs = [
        pl.BlockSpec((BQ, heads * HD), lambda i, *_: (i, 0)),
        pl.BlockSpec((HD, keys), whole),
        pl.BlockSpec((keys, HD), whole),
        pl.BlockSpec((BQ, HD), lambda i, *_: (i, 0)),
        pl.BlockSpec((1, keys), whole),
    ]
    operands = [
        lo, hi, q_docs[::BQ], q_docs[BQ - 1::BQ], k_docs[::BK], k_docs[BK - 1::BK],
        local_q, keys_t, values, jnp.broadcast_to(q_docs[:, None], (rows, HD)),
        k_docs.reshape(1, keys),
    ]
    if not first:
        in_specs += state_specs
        operands += list(state)
    if last:
        out_specs = pl.BlockSpec((BQ, heads * HD), lambda i, *_: (i, 0))
        out_shape = jax.ShapeDtypeStruct((rows, heads * HD), jnp.bfloat16)
    else:
        out_specs = state_specs
        out_shape = state_shapes
    grid_spec = pltpu.PrefetchScalarGridSpec(
        num_scalar_prefetch=6,
        grid=(rows // BQ,),
        in_specs=in_specs,
        out_specs=out_specs,
        scratch_shapes=[
            pltpu.VMEM((heads, BQ, HD), jnp.float32),
            pltpu.VMEM((heads, BQ, HD), jnp.float32),
            pltpu.VMEM((heads, BQ, HD), jnp.float32),
        ],
    )
    return pl.pallas_call(
        kernel,
        grid_spec=grid_spec,
        out_shape=out_shape,
        compiler_params=pltpu.CompilerParams(dimension_semantics=("arbitrary",)),
    )(*operands)


def on_device(queries, key_vectors, value_vectors, doc_lengths):
    head_dim = HD
    token_rows = queries.shape[0]
    query_total = queries.shape[1] // head_dim
    groups = lax.axis_size("hx")
    heads = query_total // groups
    message = jnp.concatenate(
        [
            queries.reshape(token_rows, groups, heads * head_dim),
            key_vectors.reshape(token_rows, groups, head_dim),
            value_vectors.reshape(token_rows, groups, head_dim),
        ],
        axis=2,
    ).reshape(token_rows, -1)
    arrived = lax.all_to_all(message, "hx", split_axis=1, concat_axis=0, tiled=True)
    width = heads * head_dim
    local_q = arrived[:, :width]
    own = arrived[:, width:]
    chunk_rows = local_q.shape[0]
    behind = MAXDOC // chunk_rows
    previous = [passed_along(own, TOKEN_AXES, 1)]
    per_seq = lax.axis_size("zhi")
    for distance in range(2, behind + 1):
        hop, rest = divmod(distance, per_seq)
        source = own if rest == 0 else previous[rest - 1]
        previous.append(passed_along(source, "seq", hop))
    kv_before = jnp.concatenate(previous[::-1], axis=0)

    doc_ends = jnp.cumsum(doc_lengths).astype(jnp.int32)
    chunk = lax.axis_index("seq") * per_seq + lax.axis_index("zhi")
    chunk_first = chunk * chunk_rows
    query_pos = chunk_first + jnp.arange(chunk_rows, dtype=jnp.int32)
    q_docs = document_ids(doc_ends, query_pos)
    before_rows = kv_before.shape[0]
    before_pos = chunk_first - before_rows + jnp.arange(before_rows, dtype=jnp.int32)
    before_docs = jnp.where(before_pos >= 0, document_ids(doc_ends, before_pos), -1)
    block_first = query_pos[::BQ]
    doc_first = document_starts(doc_ends, block_first)
    lo_own = jnp.maximum(doc_first - chunk_first, 0) // BK
    hi_own = (jnp.arange(chunk_rows // BQ, dtype=jnp.int32) * BQ + BQ - 1) // BK + 1
    lo_before = jnp.minimum(jnp.maximum(doc_first - (chunk_first - before_rows), 0) // BK,
                            before_rows // BK)
    hi_before = jnp.full_like(lo_before, before_rows // BK)
    state = attend(local_q, own[:, :head_dim].T, own[:, head_dim:], q_docs, q_docs,
                   lo_own.astype(jnp.int32), hi_own.astype(jnp.int32), None, heads, True, False)
    blocks = attend(local_q, kv_before[:, :head_dim].T, kv_before[:, head_dim:], q_docs,
                    before_docs, lo_before.astype(jnp.int32), hi_before.astype(jnp.int32), state,
                    heads, False, True)
    return lax.all_to_all(blocks, "hx", split_axis=0, concat_axis=1, tiled=True)


def solution(mesh):
    seq = mesh.shape["seq"]
    head = mesh.shape["head"]
    split = head // KVH
    token_mesh = Mesh(mesh.devices.reshape(seq, split, head // split), ("seq", "zhi", "hx"))
    rows = P(("seq", "zhi", "hx"), None)
    return jax.shard_map(
        on_device,
        mesh=token_mesh,
        in_specs=(rows, rows, rows, P()),
        out_specs=rows,
        check_vma=False,
    )
```

```python
import functools
import math

import jax
import jax.numpy as jnp
from jax import lax
from jax.experimental import pallas as pl
from jax.experimental.pallas import tpu as pltpu
from jax.sharding import Mesh
from jax.sharding import PartitionSpec as P

HD = 128
KVH = 8
MAXDOC = 4096
BQ = 256
BK = 512
TOKEN_AXES = ("seq", "zhi")


def passed_along(shard, axis, by):
    size = lax.axis_size(axis)
    pairs = [(i, i + by) for i in range(size) if 0 <= i + by < size]
    return lax.ppermute(shard, axis, pairs)


def document_ids(doc_ends, positions):
    return jnp.sum((doc_ends[None, :] <= positions[:, None]).astype(jnp.int32), axis=1)


def document_starts(doc_ends, positions):
    before = doc_ends[None, :] <= positions[:, None]
    return jnp.max(jnp.where(before, doc_ends[None, :], 0), axis=1)


def attention_kernel(lo_ref, hi_ref, qdf_ref, qdl_ref, kdf_ref, kdl_ref, q_ref, kt_ref, v_ref,
                     qd_ref, kd_ref, *rest, heads, causal, first, last, scaling):
    if first:
        o_refs, (m_sc, l_sc, acc_sc) = rest[:-3], rest[-3:]
    else:
        (m_in, l_in, acc_in), o_refs, (m_sc, l_sc, acc_sc) = rest[:3], rest[3:-3], rest[-3:]
    block = pl.program_id(0)
    lo = lo_ref[block]
    hi = hi_ref[block]
    q_doc_first = qdf_ref[block]
    q_single = q_doc_first == qdl_ref[block]
    lanes = acc_sc.shape[-1]
    reps = BK // lanes
    if first:
        m_sc[...] = jnp.full(m_sc.shape, -1e30, jnp.float32)
        l_sc[...] = jnp.zeros(l_sc.shape, jnp.float32)
        acc_sc[...] = jnp.zeros(acc_sc.shape, jnp.float32)
    else:
        m_sc[...] = jnp.broadcast_to(m_in[...], m_sc.shape)
        l_sc[...] = jnp.broadcast_to(l_in[...], l_sc.shape)
        acc_sc[...] = acc_in[...]

    def update(start, masked):
        keys = kt_ref[:, pl.ds(start, BK)]
        values = v_ref[pl.ds(start, BK), :]
        if masked:
            allowed = jnp.tile(qd_ref[...], (1, reps)) == kd_ref[:, pl.ds(start, BK)]
            if causal:
                rows = block * BQ + lax.broadcasted_iota(jnp.int32, (BQ, BK), 0)
                cols = start + lax.broadcasted_iota(jnp.int32, (BQ, BK), 1)
                allowed = allowed & (cols <= rows)
        for h in range(heads):
            q = q_ref[:, h * HD:(h + 1) * HD]
            s = jnp.dot(q, keys, preferred_element_type=jnp.float32) * scaling
            if masked:
                s = jnp.where(allowed, s, -1e30)
            m_prev = m_sc[h]
            m_next = jnp.maximum(m_prev, jnp.max(s, axis=-1, keepdims=True))
            e = jnp.exp(s - jnp.tile(m_next, (1, reps)))
            if masked:
                e = jnp.where(allowed, e, 0.0)
            fading = jnp.exp(m_prev - m_next)
            l_sc[h] = l_sc[h] * fading + jnp.sum(e, axis=-1, keepdims=True)
            acc_sc[h] = acc_sc[h] * fading + jnp.dot(e.astype(jnp.bfloat16), values,
                                                     preferred_element_type=jnp.float32)
            m_sc[h] = m_next

    def step(j, carry):
        start = pl.multiple_of(j * BK, BK)
        k_doc_first = kdf_ref[j]
        whole = q_single & (k_doc_first == kdl_ref[j]) & (k_doc_first == q_doc_first)
        if causal:
            whole = whole & (start + BK - 1 <= block * BQ)

        @pl.when(whole)
        def _():
            update(start, False)

        @pl.when(jnp.logical_not(whole))
        def _():
            update(start, True)

        return carry

    lax.fori_loop(lo, hi, step, 0)
    if last:
        (o_ref,) = o_refs
        for h in range(heads):
            o_ref[:, h * HD:(h + 1) * HD] = (acc_sc[h] / l_sc[h]).astype(o_ref.dtype)
    else:
        m_out, l_out, acc_out = o_refs
        m_out[...] = m_sc[:, :, 0:1]
        l_out[...] = l_sc[:, :, 0:1]
        acc_out[...] = acc_sc[...]


def attend(local_q, keys_t, values, q_docs, k_docs, lo, hi, state, heads, causal, last):
    rows = local_q.shape[0]
    keys = values.shape[0]
    first = state is None
    kernel = functools.partial(attention_kernel, heads=heads, causal=causal, first=first,
                               last=last, scaling=1.0 / math.sqrt(HD))
    per_block = lambda i, *_: (0, i, 0)
    whole = lambda i, *_: (0, 0)
    state_specs = [
        pl.BlockSpec((heads, BQ, 1), per_block),
        pl.BlockSpec((heads, BQ, 1), per_block),
        pl.BlockSpec((heads, BQ, HD), per_block),
    ]
    state_shapes = [
        jax.ShapeDtypeStruct((heads, rows, 1), jnp.float32),
        jax.ShapeDtypeStruct((heads, rows, 1), jnp.float32),
        jax.ShapeDtypeStruct((heads, rows, HD), jnp.float32),
    ]
    in_specs = [
        pl.BlockSpec((BQ, heads * HD), lambda i, *_: (i, 0)),
        pl.BlockSpec((HD, keys), whole),
        pl.BlockSpec((keys, HD), whole),
        pl.BlockSpec((BQ, HD), lambda i, *_: (i, 0)),
        pl.BlockSpec((1, keys), whole),
    ]
    operands = [
        lo, hi, q_docs[::BQ], q_docs[BQ - 1::BQ], k_docs[::BK], k_docs[BK - 1::BK],
        local_q, keys_t, values, jnp.broadcast_to(q_docs[:, None], (rows, HD)),
        k_docs.reshape(1, keys),
    ]
    if not first:
        in_specs += state_specs
        operands += list(state)
    if last:
        out_specs = pl.BlockSpec((BQ, heads * HD), lambda i, *_: (i, 0))
        out_shape = jax.ShapeDtypeStruct((rows, heads * HD), jnp.bfloat16)
    else:
        out_specs = state_specs
        out_shape = state_shapes
    grid_spec = pltpu.PrefetchScalarGridSpec(
        num_scalar_prefetch=6,
        grid=(rows // BQ,),
        in_specs=in_specs,
        out_specs=out_specs,
        scratch_shapes=[
            pltpu.VMEM((heads, BQ, HD), jnp.float32),
            pltpu.VMEM((heads, BQ, HD), jnp.float32),
            pltpu.VMEM((heads, BQ, HD), jnp.float32),
        ],
    )
    return pl.pallas_call(
        kernel,
        grid_spec=grid_spec,
        out_shape=out_shape,
        compiler_params=pltpu.CompilerParams(dimension_semantics=("arbitrary",)),
    )(*operands)


def on_device(queries, key_vectors, value_vectors, doc_lengths):
    head_dim = HD
    token_rows = queries.shape[0]
    query_total = queries.shape[1] // head_dim
    groups = lax.axis_size("hx")
    heads = query_total // groups
    message = jnp.concatenate(
        [
            queries.reshape(token_rows, groups, heads * head_dim),
            key_vectors.reshape(token_rows, groups, head_dim),
            value_vectors.reshape(token_rows, groups, head_dim),
        ],
        axis=2,
    ).reshape(token_rows, -1)
    arrived = lax.all_to_all(message, "hx", split_axis=1, concat_axis=0, tiled=True)
    width = heads * head_dim
    local_q = arrived[:, :width]
    own = arrived[:, width:]
    chunk_rows = local_q.shape[0]
    behind = MAXDOC // chunk_rows
    per_seq = lax.axis_size("zhi")
    crossed = passed_along(own, TOKEN_AXES, 1)
    two_back = passed_along(own, "seq", 2)
    one_back = passed_along(jnp.concatenate([crossed, own], axis=0), "seq", 1)
    previous = [crossed, one_back, two_back]
    kv_before = jnp.concatenate(previous[::-1], axis=0)

    doc_ends = jnp.cumsum(doc_lengths).astype(jnp.int32)
    chunk = lax.axis_index("seq") * per_seq + lax.axis_index("zhi")
    chunk_first = chunk * chunk_rows
    query_pos = chunk_first + jnp.arange(chunk_rows, dtype=jnp.int32)
    q_docs = document_ids(doc_ends, query_pos)
    before_rows = kv_before.shape[0]
    before_pos = chunk_first - before_rows + jnp.arange(before_rows, dtype=jnp.int32)
    before_docs = jnp.where(before_pos >= 0, document_ids(doc_ends, before_pos), -1)
    block_first = query_pos[::BQ]
    doc_first = document_starts(doc_ends, block_first)
    lo_own = jnp.maximum(doc_first - chunk_first, 0) // BK
    hi_own = (jnp.arange(chunk_rows // BQ, dtype=jnp.int32) * BQ + BQ - 1) // BK + 1
    lo_before = jnp.minimum(jnp.maximum(doc_first - (chunk_first - before_rows), 0) // BK,
                            before_rows // BK)
    hi_before = jnp.full_like(lo_before, before_rows // BK)
    state = attend(local_q, own[:, :head_dim].T, own[:, head_dim:], q_docs, q_docs,
                   lo_own.astype(jnp.int32), hi_own.astype(jnp.int32), None, heads, True, False)
    blocks = attend(local_q, kv_before[:, :head_dim].T, kv_before[:, head_dim:], q_docs,
                    before_docs, lo_before.astype(jnp.int32), hi_before.astype(jnp.int32), state,
                    heads, False, True)
    return lax.all_to_all(blocks, "hx", split_axis=0, concat_axis=1, tiled=True)


def solution(mesh):
    seq = mesh.shape["seq"]
    head = mesh.shape["head"]
    split = head // KVH
    token_mesh = Mesh(mesh.devices.reshape(seq, split, head // split), ("seq", "zhi", "hx"))
    rows = P(("seq", "zhi", "hx"), None)
    return jax.shard_map(
        on_device,
        mesh=token_mesh,
        in_specs=(rows, rows, rows, P()),
        out_specs=rows,
        check_vma=False,
    )
```

```python
import functools
import math

import jax
import jax.numpy as jnp
from jax import lax
from jax.experimental import pallas as pl
from jax.experimental.pallas import tpu as pltpu
from jax.sharding import Mesh
from jax.sharding import PartitionSpec as P

HD = 128
KVH = 8
MAXDOC = 4096
BQ = 256
BK = 512
TOKEN_AXES = ("seq", "zhi")


def passed_along(shard, axis, by):
    size = lax.axis_size(axis)
    pairs = [(i, i + by) for i in range(size) if 0 <= i + by < size]
    return lax.ppermute(shard, axis, pairs)


def document_ids(doc_ends, positions):
    return jnp.sum((doc_ends[None, :] <= positions[:, None]).astype(jnp.int32), axis=1)


def document_starts(doc_ends, positions):
    before = doc_ends[None, :] <= positions[:, None]
    return jnp.max(jnp.where(before, doc_ends[None, :], 0), axis=1)


def attention_kernel(lo_ref, hi_ref, qdf_ref, qdl_ref, kdf_ref, kdl_ref, q_ref, kt_ref, v_ref,
                     qd_ref, kd_ref, *rest, heads, causal, first, last, scaling):
    if first:
        o_refs, (m_sc, l_sc, acc_sc) = rest[:-3], rest[-3:]
    else:
        (m_in, l_in, acc_in), o_refs, (m_sc, l_sc, acc_sc) = rest[:3], rest[3:-3], rest[-3:]
    block = pl.program_id(0)
    lo = lo_ref[block]
    hi = hi_ref[block]
    q_doc_first = qdf_ref[block]
    q_single = q_doc_first == qdl_ref[block]
    lanes = acc_sc.shape[-1]
    reps = BK // lanes
    if first:
        m_sc[...] = jnp.full(m_sc.shape, -1e30, jnp.float32)
        l_sc[...] = jnp.zeros(l_sc.shape, jnp.float32)
        acc_sc[...] = jnp.zeros(acc_sc.shape, jnp.float32)
    else:
        m_sc[...] = jnp.broadcast_to(m_in[...], m_sc.shape)
        l_sc[...] = jnp.broadcast_to(l_in[...], l_sc.shape)
        acc_sc[...] = acc_in[...]

    def update(start, masked):
        keys = kt_ref[:, pl.ds(start, BK)]
        values = v_ref[pl.ds(start, BK), :]
        if masked:
            allowed = jnp.tile(qd_ref[...], (1, reps)) == kd_ref[:, pl.ds(start, BK)]
            if causal:
                rows = block * BQ + lax.broadcasted_iota(jnp.int32, (BQ, BK), 0)
                cols = start + lax.broadcasted_iota(jnp.int32, (BQ, BK), 1)
                allowed = allowed & (cols <= rows)
        for h in range(heads):
            q = q_ref[:, h * HD:(h + 1) * HD]
            s = jnp.dot(q, keys, preferred_element_type=jnp.float32) * scaling
            if masked:
                s = jnp.where(allowed, s, -1e30)
            m_prev = m_sc[h]
            m_next = jnp.maximum(m_prev, jnp.max(s, axis=-1, keepdims=True))
            e = jnp.exp(s - jnp.tile(m_next, (1, reps)))
            if masked:
                e = jnp.where(allowed, e, 0.0)
            fading = jnp.exp(m_prev - m_next)
            l_sc[h] = l_sc[h] * fading + jnp.sum(e, axis=-1, keepdims=True)
            acc_sc[h] = acc_sc[h] * fading + jnp.dot(e.astype(jnp.bfloat16), values,
                                                     preferred_element_type=jnp.float32)
            m_sc[h] = m_next

    def step(j, carry):
        start = pl.multiple_of(j * BK, BK)
        k_doc_first = kdf_ref[j]
        whole = q_single & (k_doc_first == kdl_ref[j]) & (k_doc_first == q_doc_first)
        if causal:
            whole = whole & (start + BK - 1 <= block * BQ)

        @pl.when(whole)
        def _():
            update(start, False)

        @pl.when(jnp.logical_not(whole))
        def _():
            update(start, True)

        return carry

    lax.fori_loop(lo, hi, step, 0)
    if last:
        (o_ref,) = o_refs
        for h in range(heads):
            o_ref[:, h * HD:(h + 1) * HD] = (acc_sc[h] / l_sc[h]).astype(o_ref.dtype)
    else:
        m_out, l_out, acc_out = o_refs
        m_out[...] = m_sc[:, :, 0:1]
        l_out[...] = l_sc[:, :, 0:1]
        acc_out[...] = acc_sc[...]


def attend(local_q, keys_t, values, q_docs, k_docs, lo, hi, state, heads, causal, last):
    rows = local_q.shape[0]
    keys = values.shape[0]
    first = state is None
    kernel = functools.partial(attention_kernel, heads=heads, causal=causal, first=first,
                               last=last, scaling=1.0 / math.sqrt(HD))
    per_block = lambda i, *_: (0, i, 0)
    whole = lambda i, *_: (0, 0)
    state_specs = [
        pl.BlockSpec((heads, BQ, 1), per_block),
        pl.BlockSpec((heads, BQ, 1), per_block),
        pl.BlockSpec((heads, BQ, HD), per_block),
    ]
    state_shapes = [
        jax.ShapeDtypeStruct((heads, rows, 1), jnp.float32),
        jax.ShapeDtypeStruct((heads, rows, 1), jnp.float32),
        jax.ShapeDtypeStruct((heads, rows, HD), jnp.float32),
    ]
    in_specs = [
        pl.BlockSpec((BQ, heads * HD), lambda i, *_: (i, 0)),
        pl.BlockSpec((HD, keys), whole),
        pl.BlockSpec((keys, HD), whole),
        pl.BlockSpec((BQ, HD), lambda i, *_: (i, 0)),
        pl.BlockSpec((1, keys), whole),
    ]
    operands = [
        lo, hi, q_docs[::BQ], q_docs[BQ - 1::BQ], k_docs[::BK], k_docs[BK - 1::BK],
        local_q, keys_t, values, jnp.broadcast_to(q_docs[:, None], (rows, HD)),
        k_docs.reshape(1, keys),
    ]
    if not first:
        in_specs += state_specs
        operands += list(state)
    if last:
        out_specs = pl.BlockSpec((BQ, heads * HD), lambda i, *_: (i, 0))
        out_shape = jax.ShapeDtypeStruct((rows, heads * HD), jnp.bfloat16)
    else:
        out_specs = state_specs
        out_shape = state_shapes
    grid_spec = pltpu.PrefetchScalarGridSpec(
        num_scalar_prefetch=6,
        grid=(rows // BQ,),
        in_specs=in_specs,
        out_specs=out_specs,
        scratch_shapes=[
            pltpu.VMEM((heads, BQ, HD), jnp.float32),
            pltpu.VMEM((heads, BQ, HD), jnp.float32),
            pltpu.VMEM((heads, BQ, HD), jnp.float32),
        ],
    )
    return pl.pallas_call(
        kernel,
        grid_spec=grid_spec,
        out_shape=out_shape,
        compiler_params=pltpu.CompilerParams(dimension_semantics=("arbitrary",)),
    )(*operands)


def on_device(queries, key_vectors, value_vectors, doc_lengths):
    head_dim = HD
    token_rows = queries.shape[0]
    query_total = queries.shape[1] // head_dim
    groups = lax.axis_size("hx")
    heads = query_total // groups
    message = jnp.concatenate(
        [
            queries.reshape(token_rows, groups, heads * head_dim),
            key_vectors.reshape(token_rows, groups, head_dim),
            value_vectors.reshape(token_rows, groups, head_dim),
        ],
        axis=2,
    ).reshape(token_rows, -1)
    arrived = lax.all_to_all(message, "hx", split_axis=1, concat_axis=0, tiled=True)
    width = heads * head_dim
    local_q = arrived[:, :width]
    own = arrived[:, width:]
    chunk_rows = local_q.shape[0]
    behind = MAXDOC // chunk_rows
    per_seq = lax.axis_size("zhi")
    previous = []
    for distance in range(1, behind + 1):
        hop, rest = divmod(distance, per_seq)
        if rest == 0:
            previous.append(passed_along(own, "seq", hop))
        else:
            previous.append(passed_along(own, TOKEN_AXES, distance))
    kv_before = jnp.concatenate(previous[::-1], axis=0)

    doc_ends = jnp.cumsum(doc_lengths).astype(jnp.int32)
    chunk = lax.axis_index("seq") * per_seq + lax.axis_index("zhi")
    chunk_first = chunk * chunk_rows
    query_pos = chunk_first + jnp.arange(chunk_rows, dtype=jnp.int32)
    q_docs = document_ids(doc_ends, query_pos)
    before_rows = kv_before.shape[0]
    before_pos = chunk_first - before_rows + jnp.arange(before_rows, dtype=jnp.int32)
    before_docs = jnp.where(before_pos >= 0, document_ids(doc_ends, before_pos), -1)
    block_first = query_pos[::BQ]
    doc_first = document_starts(doc_ends, block_first)
    lo_own = jnp.maximum(doc_first - chunk_first, 0) // BK
    hi_own = (jnp.arange(chunk_rows // BQ, dtype=jnp.int32) * BQ + BQ - 1) // BK + 1
    lo_before = jnp.minimum(jnp.maximum(doc_first - (chunk_first - before_rows), 0) // BK,
                            before_rows // BK)
    hi_before = jnp.full_like(lo_before, before_rows // BK)
    state = attend(local_q, own[:, :head_dim].T, own[:, head_dim:], q_docs, q_docs,
                   lo_own.astype(jnp.int32), hi_own.astype(jnp.int32), None, heads, True, False)
    blocks = attend(local_q, kv_before[:, :head_dim].T, kv_before[:, head_dim:], q_docs,
                    before_docs, lo_before.astype(jnp.int32), hi_before.astype(jnp.int32), state,
                    heads, False, True)
    return lax.all_to_all(blocks, "hx", split_axis=0, concat_axis=1, tiled=True)


def solution(mesh):
    seq = mesh.shape["seq"]
    head = mesh.shape["head"]
    split = head // KVH
    token_mesh = Mesh(mesh.devices.reshape(seq, split, head // split), ("seq", "zhi", "hx"))
    rows = P(("seq", "zhi", "hx"), None)
    return jax.shard_map(
        on_device,
        mesh=token_mesh,
        in_specs=(rows, rows, rows, P()),
        out_specs=rows,
        check_vma=False,
    )
```

```python
import functools
import math

import jax
import jax.numpy as jnp
from jax import lax
from jax.experimental import pallas as pl
from jax.experimental.pallas import tpu as pltpu
from jax.sharding import Mesh
from jax.sharding import PartitionSpec as P

HD = 128
KVH = 8
MAXDOC = 4096
BQ = 256
BK = 512
TOKEN_AXES = ("seq", "zhi")


def passed_along(shard, axis, by):
    size = lax.axis_size(axis)
    pairs = [(i, i + by) for i in range(size) if 0 <= i + by < size]
    return lax.ppermute(shard, axis, pairs)


def document_ids(doc_ends, positions):
    return jnp.sum((doc_ends[None, :] <= positions[:, None]).astype(jnp.int32), axis=1)


def document_starts(doc_ends, positions):
    before = doc_ends[None, :] <= positions[:, None]
    return jnp.max(jnp.where(before, doc_ends[None, :], 0), axis=1)


def attention_kernel(lo_ref, hi_ref, qdf_ref, qdl_ref, kdf_ref, kdl_ref, q_ref, kt_ref, v_ref,
                     qd_ref, kd_ref, *rest, heads, causal, first, last, scaling):
    if first:
        o_refs, (m_sc, l_sc, acc_sc) = rest[:-3], rest[-3:]
    else:
        (m_in, l_in, acc_in), o_refs, (m_sc, l_sc, acc_sc) = rest[:3], rest[3:-3], rest[-3:]
    block = pl.program_id(0)
    lo = lo_ref[block]
    hi = hi_ref[block]
    q_doc_first = qdf_ref[block]
    q_single = q_doc_first == qdl_ref[block]
    lanes = acc_sc.shape[-1]
    reps = BK // lanes
    if first:
        m_sc[...] = jnp.full(m_sc.shape, -1e30, jnp.float32)
        l_sc[...] = jnp.zeros(l_sc.shape, jnp.float32)
        acc_sc[...] = jnp.zeros(acc_sc.shape, jnp.float32)
    else:
        m_sc[...] = jnp.broadcast_to(m_in[...], m_sc.shape)
        l_sc[...] = jnp.broadcast_to(l_in[...], l_sc.shape)
        acc_sc[...] = acc_in[...]

    def update(start, masked):
        keys = kt_ref[:, pl.ds(start, BK)]
        values = v_ref[pl.ds(start, BK), :]
        if masked:
            allowed = jnp.tile(qd_ref[...], (1, reps)) == kd_ref[:, pl.ds(start, BK)]
            if causal:
                rows = block * BQ + lax.broadcasted_iota(jnp.int32, (BQ, BK), 0)
                cols = start + lax.broadcasted_iota(jnp.int32, (BQ, BK), 1)
                allowed = allowed & (cols <= rows)
        for h in range(heads):
            q = q_ref[:, h * HD:(h + 1) * HD]
            s = jnp.dot(q, keys, preferred_element_type=jnp.float32) * scaling
            if masked:
                s = jnp.where(allowed, s, -1e30)
            m_prev = m_sc[h]
            m_next = jnp.maximum(m_prev, jnp.max(s, axis=-1, keepdims=True))
            e = jnp.exp(s - jnp.tile(m_next, (1, reps)))
            if masked:
                e = jnp.where(allowed, e, 0.0)
            fading = jnp.exp(m_prev - m_next)
            l_sc[h] = l_sc[h] * fading + jnp.sum(e, axis=-1, keepdims=True)
            acc_sc[h] = acc_sc[h] * fading + jnp.dot(e.astype(jnp.bfloat16), values,
                                                     preferred_element_type=jnp.float32)
            m_sc[h] = m_next

    def step(j, carry):
        start = pl.multiple_of(j * BK, BK)
        k_doc_first = kdf_ref[j]
        whole = q_single & (k_doc_first == kdl_ref[j]) & (k_doc_first == q_doc_first)
        if causal:
            whole = whole & (start + BK - 1 <= block * BQ)

        @pl.when(whole)
        def _():
            update(start, False)

        @pl.when(jnp.logical_not(whole))
        def _():
            update(start, True)

        return carry

    lax.fori_loop(lo, hi, step, 0)
    if last:
        (o_ref,) = o_refs
        for h in range(heads):
            o_ref[:, h * HD:(h + 1) * HD] = (acc_sc[h] / l_sc[h]).astype(o_ref.dtype)
    else:
        m_out, l_out, acc_out = o_refs
        m_out[...] = m_sc[:, :, 0:1]
        l_out[...] = l_sc[:, :, 0:1]
        acc_out[...] = acc_sc[...]


def attend(local_q, keys_t, values, q_docs, k_docs, lo, hi, state, heads, causal, last):
    rows = local_q.shape[0]
    keys = values.shape[0]
    first = state is None
    kernel = functools.partial(attention_kernel, heads=heads, causal=causal, first=first,
                               last=last, scaling=1.0 / math.sqrt(HD))
    per_block = lambda i, *_: (0, i, 0)
    whole = lambda i, *_: (0, 0)
    state_specs = [
        pl.BlockSpec((heads, BQ, 1), per_block),
        pl.BlockSpec((heads, BQ, 1), per_block),
        pl.BlockSpec((heads, BQ, HD), per_block),
    ]
    state_shapes = [
        jax.ShapeDtypeStruct((heads, rows, 1), jnp.float32),
        jax.ShapeDtypeStruct((heads, rows, 1), jnp.float32),
        jax.ShapeDtypeStruct((heads, rows, HD), jnp.float32),
    ]
    in_specs = [
        pl.BlockSpec((BQ, heads * HD), lambda i, *_: (i, 0)),
        pl.BlockSpec((HD, keys), whole),
        pl.BlockSpec((keys, HD), whole),
        pl.BlockSpec((BQ, HD), lambda i, *_: (i, 0)),
        pl.BlockSpec((1, keys), whole),
    ]
    operands = [
        lo, hi, q_docs[::BQ], q_docs[BQ - 1::BQ], k_docs[::BK], k_docs[BK - 1::BK],
        local_q, keys_t, values, jnp.broadcast_to(q_docs[:, None], (rows, HD)),
        k_docs.reshape(1, keys),
    ]
    if not first:
        in_specs += state_specs
        operands += list(state)
    if last:
        out_specs = pl.BlockSpec((BQ, heads * HD), lambda i, *_: (i, 0))
        out_shape = jax.ShapeDtypeStruct((rows, heads * HD), jnp.bfloat16)
    else:
        out_specs = state_specs
        out_shape = state_shapes
    grid_spec = pltpu.PrefetchScalarGridSpec(
        num_scalar_prefetch=6,
        grid=(rows // BQ,),
        in_specs=in_specs,
        out_specs=out_specs,
        scratch_shapes=[
            pltpu.VMEM((heads, BQ, HD), jnp.float32),
            pltpu.VMEM((heads, BQ, HD), jnp.float32),
            pltpu.VMEM((heads, BQ, HD), jnp.float32),
        ],
    )
    return pl.pallas_call(
        kernel,
        grid_spec=grid_spec,
        out_shape=out_shape,
        compiler_params=pltpu.CompilerParams(dimension_semantics=("arbitrary",)),
    )(*operands)


def on_device(queries, key_vectors, value_vectors, doc_lengths):
    head_dim = HD
    token_rows = queries.shape[0]
    query_total = queries.shape[1] // head_dim
    groups = lax.axis_size("hx")
    heads = query_total // groups
    message = jnp.concatenate(
        [
            queries.reshape(token_rows, groups, heads * head_dim),
            key_vectors.reshape(token_rows, groups, head_dim),
            value_vectors.reshape(token_rows, groups, head_dim),
        ],
        axis=2,
    ).reshape(token_rows, -1)
    arrived = lax.all_to_all(message, "hx", split_axis=1, concat_axis=0, tiled=True)
    width = heads * head_dim
    local_q = arrived[:, :width]
    own = arrived[:, width:]
    chunk_rows = local_q.shape[0]
    behind = MAXDOC // chunk_rows
    per_seq = lax.axis_size("zhi")
    previous = []
    for distance in range(1, behind + 1):
        hop, rest = divmod(distance, per_seq)
        if rest == 0:
            previous.append(passed_along(own, "seq", hop))
        else:
            previous.append(passed_along(own, TOKEN_AXES, distance))
    doc_ends = jnp.cumsum(doc_lengths).astype(jnp.int32)
    chunk = lax.axis_index("seq") * per_seq + lax.axis_index("zhi")
    chunk_first = chunk * chunk_rows
    offsets = jnp.arange(chunk_rows, dtype=jnp.int32)
    query_pos = chunk_first + offsets
    q_docs = document_ids(doc_ends, query_pos)
    doc_first = document_starts(doc_ends, query_pos[::BQ])
    lo_own = jnp.maximum(doc_first - chunk_first, 0) // BK
    hi_own = (jnp.arange(chunk_rows // BQ, dtype=jnp.int32) * BQ + BQ - 1) // BK + 1
    state = attend(local_q, own[:, :head_dim].T, own[:, head_dim:], q_docs, q_docs,
                   lo_own.astype(jnp.int32), hi_own.astype(jnp.int32), None, heads, True, False)
    along_seq = [d for d in range(behind, 0, -1) if d % per_seq == 0]
    crossing = [d for d in range(behind, 0, -1) if d % per_seq != 0]
    for index, distances in enumerate([along_seq, crossing]):
        parts = [previous[d - 1] for d in distances]
        if index:
            parts, state = lax.optimization_barrier((parts, state))
        kv = jnp.concatenate(parts, axis=0)
        key_pos = jnp.concatenate([chunk_first - d * chunk_rows + offsets for d in distances])
        key_docs = jnp.where(key_pos >= 0, document_ids(doc_ends, key_pos), -1)
        block_last = key_pos[BK - 1::BK]
        lo = jnp.sum((block_last[None, :] < doc_first[:, None]).astype(jnp.int32), axis=1)
        hi = jnp.full_like(lo, block_last.shape[0])
        state = attend(local_q, kv[:, :head_dim].T, kv[:, head_dim:], q_docs, key_docs,
                       lo.astype(jnp.int32), hi.astype(jnp.int32), state, heads, False,
                       index == 1)
    blocks = state
    return lax.all_to_all(blocks, "hx", split_axis=0, concat_axis=1, tiled=True)


def solution(mesh):
    seq = mesh.shape["seq"]
    head = mesh.shape["head"]
    split = head // KVH
    token_mesh = Mesh(mesh.devices.reshape(seq, split, head // split), ("seq", "zhi", "hx"))
    rows = P(("seq", "zhi", "hx"), None)
    return jax.shard_map(
        on_device,
        mesh=token_mesh,
        in_specs=(rows, rows, rows, P()),
        out_specs=rows,
        check_vma=False,
    )
```

```python
import functools
import math

import jax
import jax.numpy as jnp
from jax import lax
from jax.experimental import pallas as pl
from jax.experimental.pallas import tpu as pltpu
from jax.sharding import Mesh
from jax.sharding import PartitionSpec as P

HD = 128
KVH = 8
MAXDOC = 4096
BQ = 256
BK = 512
TOKEN_AXES = ("seq", "zhi")


def passed_along(shard, axis, by):
    size = lax.axis_size(axis)
    pairs = [(i, i + by) for i in range(size) if 0 <= i + by < size]
    return lax.ppermute(shard, axis, pairs)


def document_ids(doc_ends, positions):
    return jnp.sum((doc_ends[None, :] <= positions[:, None]).astype(jnp.int32), axis=1)


def document_starts(doc_ends, positions):
    before = doc_ends[None, :] <= positions[:, None]
    return jnp.max(jnp.where(before, doc_ends[None, :], 0), axis=1)


def attention_kernel(lo_ref, hi_ref, qdf_ref, qdl_ref, kdf_ref, kdl_ref, q_ref, kt_ref, v_ref,
                     qd_ref, kd_ref, *rest, heads, causal, first, last, scaling):
    if first:
        o_refs, (m_sc, l_sc, acc_sc) = rest[:-3], rest[-3:]
    else:
        (m_in, l_in, acc_in), o_refs, (m_sc, l_sc, acc_sc) = rest[:3], rest[3:-3], rest[-3:]
    block = pl.program_id(0)
    lo = lo_ref[block]
    hi = hi_ref[block]
    q_doc_first = qdf_ref[block]
    q_single = q_doc_first == qdl_ref[block]
    lanes = acc_sc.shape[-1]
    reps = BK // lanes
    if first:
        m_sc[...] = jnp.full(m_sc.shape, -1e30, jnp.float32)
        l_sc[...] = jnp.zeros(l_sc.shape, jnp.float32)
        acc_sc[...] = jnp.zeros(acc_sc.shape, jnp.float32)
    else:
        m_sc[...] = jnp.broadcast_to(m_in[...], m_sc.shape)
        l_sc[...] = jnp.broadcast_to(l_in[...], l_sc.shape)
        acc_sc[...] = acc_in[...]

    def update(start, masked):
        keys = kt_ref[:, pl.ds(start, BK)]
        values = v_ref[pl.ds(start, BK), :]
        if masked:
            allowed = jnp.tile(qd_ref[...], (1, reps)) == kd_ref[:, pl.ds(start, BK)]
            if causal:
                rows = block * BQ + lax.broadcasted_iota(jnp.int32, (BQ, BK), 0)
                cols = start + lax.broadcasted_iota(jnp.int32, (BQ, BK), 1)
                allowed = allowed & (cols <= rows)
        for h in range(heads):
            q = q_ref[:, h * HD:(h + 1) * HD]
            s = jnp.dot(q, keys, preferred_element_type=jnp.float32) * scaling
            if masked:
                s = jnp.where(allowed, s, -1e30)
            m_prev = m_sc[h]
            m_next = jnp.maximum(m_prev, jnp.max(s, axis=-1, keepdims=True))
            e = jnp.exp(s - jnp.tile(m_next, (1, reps)))
            if masked:
                e = jnp.where(allowed, e, 0.0)
            fading = jnp.exp(m_prev - m_next)
            l_sc[h] = l_sc[h] * fading + jnp.sum(e, axis=-1, keepdims=True)
            acc_sc[h] = acc_sc[h] * fading + jnp.dot(e.astype(jnp.bfloat16), values,
                                                     preferred_element_type=jnp.float32)
            m_sc[h] = m_next

    def step(j, carry):
        start = pl.multiple_of(j * BK, BK)
        k_doc_first = kdf_ref[j]
        whole = q_single & (k_doc_first == kdl_ref[j]) & (k_doc_first == q_doc_first)
        if causal:
            whole = whole & (start + BK - 1 <= block * BQ)

        @pl.when(whole)
        def _():
            update(start, False)

        @pl.when(jnp.logical_not(whole))
        def _():
            update(start, True)

        return carry

    lax.fori_loop(lo, hi, step, 0)
    if last:
        (o_ref,) = o_refs
        for h in range(heads):
            o_ref[:, h * HD:(h + 1) * HD] = (acc_sc[h] / l_sc[h]).astype(o_ref.dtype)
    else:
        m_out, l_out, acc_out = o_refs
        m_out[...] = m_sc[:, :, 0:1]
        l_out[...] = l_sc[:, :, 0:1]
        acc_out[...] = acc_sc[...]


def attend(local_q, keys_t, values, q_docs, k_docs, lo, hi, state, heads, causal, last):
    rows = local_q.shape[0]
    keys = values.shape[0]
    first = state is None
    kernel = functools.partial(attention_kernel, heads=heads, causal=causal, first=first,
                               last=last, scaling=1.0 / math.sqrt(HD))
    per_block = lambda i, *_: (0, i, 0)
    whole = lambda i, *_: (0, 0)
    state_specs = [
        pl.BlockSpec((heads, BQ, 1), per_block),
        pl.BlockSpec((heads, BQ, 1), per_block),
        pl.BlockSpec((heads, BQ, HD), per_block),
    ]
    state_shapes = [
        jax.ShapeDtypeStruct((heads, rows, 1), jnp.float32),
        jax.ShapeDtypeStruct((heads, rows, 1), jnp.float32),
        jax.ShapeDtypeStruct((heads, rows, HD), jnp.float32),
    ]
    in_specs = [
        pl.BlockSpec((BQ, heads * HD), lambda i, *_: (i, 0)),
        pl.BlockSpec((HD, keys), whole),
        pl.BlockSpec((keys, HD), whole),
        pl.BlockSpec((BQ, HD), lambda i, *_: (i, 0)),
        pl.BlockSpec((1, keys), whole),
    ]
    operands = [
        lo, hi, q_docs[::BQ], q_docs[BQ - 1::BQ], k_docs[::BK], k_docs[BK - 1::BK],
        local_q, keys_t, values, jnp.broadcast_to(q_docs[:, None], (rows, HD)),
        k_docs.reshape(1, keys),
    ]
    if not first:
        in_specs += state_specs
        operands += list(state)
    if last:
        out_specs = pl.BlockSpec((BQ, heads * HD), lambda i, *_: (i, 0))
        out_shape = jax.ShapeDtypeStruct((rows, heads * HD), jnp.bfloat16)
    else:
        out_specs = state_specs
        out_shape = state_shapes
    grid_spec = pltpu.PrefetchScalarGridSpec(
        num_scalar_prefetch=6,
        grid=(rows // BQ,),
        in_specs=in_specs,
        out_specs=out_specs,
        scratch_shapes=[
            pltpu.VMEM((heads, BQ, HD), jnp.float32),
            pltpu.VMEM((heads, BQ, HD), jnp.float32),
            pltpu.VMEM((heads, BQ, HD), jnp.float32),
        ],
    )
    return pl.pallas_call(
        kernel,
        grid_spec=grid_spec,
        out_shape=out_shape,
        compiler_params=pltpu.CompilerParams(dimension_semantics=("arbitrary",)),
    )(*operands)


def on_device(queries, key_vectors, value_vectors, doc_lengths):
    head_dim = HD
    token_rows = queries.shape[0]
    query_total = queries.shape[1] // head_dim
    groups = lax.axis_size("hx")
    heads = query_total // groups
    message = jnp.concatenate(
        [
            queries.reshape(token_rows, groups, heads * head_dim),
            key_vectors.reshape(token_rows, groups, head_dim),
            value_vectors.reshape(token_rows, groups, head_dim),
        ],
        axis=2,
    ).reshape(token_rows, -1)
    arrived = lax.all_to_all(message, "hx", split_axis=1, concat_axis=0, tiled=True)
    width = heads * head_dim
    local_q = arrived[:, :width]
    own = arrived[:, width:]
    chunk_rows = local_q.shape[0]
    behind = MAXDOC // chunk_rows
    per_seq = lax.axis_size("zhi")
    crossed = passed_along(own, TOKEN_AXES, 1)
    along_seq = {hop * per_seq: passed_along(own, "seq", hop) for hop in range(1, behind // per_seq + 1)}
    doc_ends = jnp.cumsum(doc_lengths).astype(jnp.int32)
    chunk = lax.axis_index("seq") * per_seq + lax.axis_index("zhi")
    chunk_first = chunk * chunk_rows
    offsets = jnp.arange(chunk_rows, dtype=jnp.int32)
    query_pos = chunk_first + offsets
    q_docs = document_ids(doc_ends, query_pos)
    doc_first = document_starts(doc_ends, query_pos[::BQ])
    lo_own = jnp.maximum(doc_first - chunk_first, 0) // BK
    hi_own = (jnp.arange(chunk_rows // BQ, dtype=jnp.int32) * BQ + BQ - 1) // BK + 1
    state = attend(local_q, own[:, :head_dim].T, own[:, head_dim:], q_docs, q_docs,
                   lo_own.astype(jnp.int32), hi_own.astype(jnp.int32), None, heads, True, False)

    def attend_chunks(parts, distances, state, last):
        kv = jnp.concatenate(parts, axis=0)
        key_pos = jnp.concatenate([chunk_first - d * chunk_rows + offsets for d in distances])
        key_docs = jnp.where(key_pos >= 0, document_ids(doc_ends, key_pos), -1)
        block_last = key_pos[BK - 1::BK]
        lo = jnp.sum((block_last[None, :] < doc_first[:, None]).astype(jnp.int32), axis=1)
        hi = jnp.full_like(lo, block_last.shape[0])
        return attend(local_q, kv[:, :head_dim].T, kv[:, head_dim:], q_docs, key_docs,
                      lo.astype(jnp.int32), hi.astype(jnp.int32), state, heads, False, last)

    far = sorted(along_seq, reverse=True)
    state = attend_chunks([along_seq[d] for d in far], far, state, False)
    crossed, state = lax.optimization_barrier((crossed, state))
    relayed = passed_along(crossed, "seq", 1)
    state = attend_chunks([crossed], [1], state, False)
    relayed, state = lax.optimization_barrier((relayed, state))
    state = attend_chunks([relayed], [per_seq + 1], state, True)
    blocks = state
    return lax.all_to_all(blocks, "hx", split_axis=0, concat_axis=1, tiled=True)


def solution(mesh):
    seq = mesh.shape["seq"]
    head = mesh.shape["head"]
    split = head // KVH
    token_mesh = Mesh(mesh.devices.reshape(seq, split, head // split), ("seq", "zhi", "hx"))
    rows = P(("seq", "zhi", "hx"), None)
    return jax.shard_map(
        on_device,
        mesh=token_mesh,
        in_specs=(rows, rows, rows, P()),
        out_specs=rows,
        check_vma=False,
    )
```

```python
import functools
import math

import jax
import jax.numpy as jnp
from jax import lax
from jax.experimental import pallas as pl
from jax.experimental.pallas import tpu as pltpu
from jax.sharding import Mesh
from jax.sharding import PartitionSpec as P

HD = 128
KVH = 8
MAXDOC = 4096
BQ = 256
BK = 512
TOKEN_AXES = ("seq", "zhi")


def passed_along(shard, axis, by):
    size = lax.axis_size(axis)
    pairs = [(i, i + by) for i in range(size) if 0 <= i + by < size]
    return lax.ppermute(shard, axis, pairs)


def document_ids(doc_ends, positions):
    return jnp.sum((doc_ends[None, :] <= positions[:, None]).astype(jnp.int32), axis=1)


def document_starts(doc_ends, positions):
    before = doc_ends[None, :] <= positions[:, None]
    return jnp.max(jnp.where(before, doc_ends[None, :], 0), axis=1)


def attention_kernel(lo_ref, hi_ref, qdf_ref, qdl_ref, kdf_ref, kdl_ref, q_ref, kt_ref, v_ref,
                     qd_ref, kd_ref, *rest, heads, causal, first, last, scaling):
    if first:
        o_refs, (m_sc, l_sc, acc_sc) = rest[:-3], rest[-3:]
    else:
        (m_in, l_in, acc_in), o_refs, (m_sc, l_sc, acc_sc) = rest[:3], rest[3:-3], rest[-3:]
    block = pl.program_id(0)
    lo = lo_ref[block]
    hi = hi_ref[block]
    q_doc_first = qdf_ref[block]
    q_single = q_doc_first == qdl_ref[block]
    lanes = acc_sc.shape[-1]
    reps = BK // lanes
    if first:
        m_sc[...] = jnp.full(m_sc.shape, -1e30, jnp.float32)
        l_sc[...] = jnp.zeros(l_sc.shape, jnp.float32)
        acc_sc[...] = jnp.zeros(acc_sc.shape, jnp.float32)
    else:
        m_sc[...] = jnp.broadcast_to(m_in[...], m_sc.shape)
        l_sc[...] = jnp.broadcast_to(l_in[...], l_sc.shape)
        acc_sc[...] = acc_in[...]

    def update(start, masked):
        keys = kt_ref[:, pl.ds(start, BK)]
        values = v_ref[pl.ds(start, BK), :]
        if masked:
            allowed = jnp.tile(qd_ref[...], (1, reps)) == kd_ref[:, pl.ds(start, BK)]
            if causal:
                rows = block * BQ + lax.broadcasted_iota(jnp.int32, (BQ, BK), 0)
                cols = start + lax.broadcasted_iota(jnp.int32, (BQ, BK), 1)
                allowed = allowed & (cols <= rows)
        for h in range(heads):
            q = q_ref[:, h * HD:(h + 1) * HD]
            s = jnp.dot(q, keys, preferred_element_type=jnp.float32) * scaling
            if masked:
                s = jnp.where(allowed, s, -1e30)
            pieces = [s[:, i * lanes:(i + 1) * lanes] for i in range(reps)]
            widest = pieces[0]
            for piece in pieces[1:]:
                widest = jnp.maximum(widest, piece)
            m_prev = m_sc[h]
            m_next = jnp.maximum(m_prev, jnp.max(widest, axis=-1, keepdims=True))
            exps = [jnp.exp2(piece - m_next) for piece in pieces]
            if masked:
                exps = [jnp.where(allowed[:, i * lanes:(i + 1) * lanes], e, 0.0)
                        for i, e in enumerate(exps)]
            total = exps[0]
            for e in exps[1:]:
                total = total + e
            fading = jnp.exp2(m_prev - m_next)
            l_sc[h] = l_sc[h] * fading + jnp.sum(total, axis=-1, keepdims=True)
            e = jnp.concatenate(exps, axis=1).astype(jnp.bfloat16)
            acc_sc[h] = acc_sc[h] * fading + jnp.dot(e, values, preferred_element_type=jnp.float32)
            m_sc[h] = m_next

    def step(j, carry):
        start = pl.multiple_of(j * BK, BK)
        k_doc_first = kdf_ref[j]
        whole = q_single & (k_doc_first == kdl_ref[j]) & (k_doc_first == q_doc_first)
        if causal:
            whole = whole & (start + BK - 1 <= block * BQ)

        @pl.when(whole)
        def _():
            update(start, False)

        @pl.when(jnp.logical_not(whole))
        def _():
            update(start, True)

        return carry

    lax.fori_loop(lo, hi, step, 0)
    if last:
        (o_ref,) = o_refs
        for h in range(heads):
            o_ref[:, h * HD:(h + 1) * HD] = (acc_sc[h] / l_sc[h]).astype(o_ref.dtype)
    else:
        m_out, l_out, acc_out = o_refs
        m_out[...] = m_sc[:, :, 0:1]
        l_out[...] = l_sc[:, :, 0:1]
        acc_out[...] = acc_sc[...]


def attend(local_q, keys_t, values, q_docs, k_docs, lo, hi, state, heads, causal, last):
    rows = local_q.shape[0]
    keys = values.shape[0]
    first = state is None
    kernel = functools.partial(attention_kernel, heads=heads, causal=causal, first=first,
                               last=last, scaling=math.log2(math.e) / math.sqrt(HD))
    per_block = lambda i, *_: (0, i, 0)
    whole = lambda i, *_: (0, 0)
    state_specs = [
        pl.BlockSpec((heads, BQ, 1), per_block),
        pl.BlockSpec((heads, BQ, 1), per_block),
        pl.BlockSpec((heads, BQ, HD), per_block),
    ]
    state_shapes = [
        jax.ShapeDtypeStruct((heads, rows, 1), jnp.float32),
        jax.ShapeDtypeStruct((heads, rows, 1), jnp.float32),
        jax.ShapeDtypeStruct((heads, rows, HD), jnp.float32),
    ]
    in_specs = [
        pl.BlockSpec((BQ, heads * HD), lambda i, *_: (i, 0)),
        pl.BlockSpec((HD, keys), whole),
        pl.BlockSpec((keys, HD), whole),
        pl.BlockSpec((BQ, HD), lambda i, *_: (i, 0)),
        pl.BlockSpec((1, keys), whole),
    ]
    operands = [
        lo, hi, q_docs[::BQ], q_docs[BQ - 1::BQ], k_docs[::BK], k_docs[BK - 1::BK],
        local_q, keys_t, values, jnp.broadcast_to(q_docs[:, None], (rows, HD)),
        k_docs.reshape(1, keys),
    ]
    if not first:
        in_specs += state_specs
        operands += list(state)
    if last:
        out_specs = pl.BlockSpec((BQ, heads * HD), lambda i, *_: (i, 0))
        out_shape = jax.ShapeDtypeStruct((rows, heads * HD), jnp.bfloat16)
    else:
        out_specs = state_specs
        out_shape = state_shapes
    grid_spec = pltpu.PrefetchScalarGridSpec(
        num_scalar_prefetch=6,
        grid=(rows // BQ,),
        in_specs=in_specs,
        out_specs=out_specs,
        scratch_shapes=[
            pltpu.VMEM((heads, BQ, HD), jnp.float32),
            pltpu.VMEM((heads, BQ, HD), jnp.float32),
            pltpu.VMEM((heads, BQ, HD), jnp.float32),
        ],
    )
    return pl.pallas_call(
        kernel,
        grid_spec=grid_spec,
        out_shape=out_shape,
        compiler_params=pltpu.CompilerParams(dimension_semantics=("arbitrary",)),
    )(*operands)


def on_device(queries, key_vectors, value_vectors, doc_lengths):
    head_dim = HD
    token_rows = queries.shape[0]
    query_total = queries.shape[1] // head_dim
    groups = lax.axis_size("hx")
    heads = query_total // groups
    message = jnp.concatenate(
        [
            queries.reshape(token_rows, groups, heads * head_dim),
            key_vectors.reshape(token_rows, groups, head_dim),
            value_vectors.reshape(token_rows, groups, head_dim),
        ],
        axis=2,
    ).reshape(token_rows, -1)
    arrived = lax.all_to_all(message, "hx", split_axis=1, concat_axis=0, tiled=True)
    width = heads * head_dim
    local_q = arrived[:, :width]
    own = arrived[:, width:]
    chunk_rows = local_q.shape[0]
    behind = MAXDOC // chunk_rows
    per_seq = lax.axis_size("zhi")
    crossed = passed_along(own, TOKEN_AXES, 1)
    along_seq = {hop * per_seq: passed_along(own, "seq", hop) for hop in range(1, behind // per_seq + 1)}
    doc_ends = jnp.cumsum(doc_lengths).astype(jnp.int32)
    chunk = lax.axis_index("seq") * per_seq + lax.axis_index("zhi")
    chunk_first = chunk * chunk_rows
    offsets = jnp.arange(chunk_rows, dtype=jnp.int32)
    query_pos = chunk_first + offsets
    q_docs = document_ids(doc_ends, query_pos)
    doc_first = document_starts(doc_ends, query_pos[::BQ])
    lo_own = jnp.maximum(doc_first - chunk_first, 0) // BK
    hi_own = (jnp.arange(chunk_rows // BQ, dtype=jnp.int32) * BQ + BQ - 1) // BK + 1
    state = attend(local_q, own[:, :head_dim].T, own[:, head_dim:], q_docs, q_docs,
                   lo_own.astype(jnp.int32), hi_own.astype(jnp.int32), None, heads, True, False)

    def attend_chunks(parts, distances, state, last):
        kv = jnp.concatenate(parts, axis=0)
        key_pos = jnp.concatenate([chunk_first - d * chunk_rows + offsets for d in distances])
        key_docs = jnp.where(key_pos >= 0, document_ids(doc_ends, key_pos), -1)
        block_last = key_pos[BK - 1::BK]
        lo = jnp.sum((block_last[None, :] < doc_first[:, None]).astype(jnp.int32), axis=1)
        hi = jnp.full_like(lo, block_last.shape[0])
        return attend(local_q, kv[:, :head_dim].T, kv[:, head_dim:], q_docs, key_docs,
                      lo.astype(jnp.int32), hi.astype(jnp.int32), state, heads, False, last)

    far = sorted(along_seq, reverse=True)
    state = attend_chunks([along_seq[d] for d in far], far, state, False)
    crossed, state = lax.optimization_barrier((crossed, state))
    relayed = passed_along(crossed, "seq", 1)
    state = attend_chunks([crossed], [1], state, False)
    relayed, state = lax.optimization_barrier((relayed, state))
    state = attend_chunks([relayed], [per_seq + 1], state, True)
    blocks = state
    return lax.all_to_all(blocks, "hx", split_axis=0, concat_axis=1, tiled=True)


def solution(mesh):
    seq = mesh.shape["seq"]
    head = mesh.shape["head"]
    split = head // KVH
    token_mesh = Mesh(mesh.devices.reshape(seq, split, head // split), ("seq", "zhi", "hx"))
    rows = P(("seq", "zhi", "hx"), None)
    return jax.shard_map(
        on_device,
        mesh=token_mesh,
        in_specs=(rows, rows, rows, P()),
        out_specs=rows,
        check_vma=False,
    )
```

```python
import functools
import math

import jax
import jax.numpy as jnp
from jax import lax
from jax.experimental import pallas as pl
from jax.experimental.pallas import tpu as pltpu
from jax.sharding import Mesh
from jax.sharding import PartitionSpec as P

HD = 128
KVH = 8
MAXDOC = 4096
BQ = 256
BK = 512
TOKEN_AXES = ("seq", "zhi")


def passed_along(shard, axis, by):
    size = lax.axis_size(axis)
    pairs = [(i, i + by) for i in range(size) if 0 <= i + by < size]
    return lax.ppermute(shard, axis, pairs)


def document_ids(doc_ends, positions):
    return jnp.sum((doc_ends[None, :] <= positions[:, None]).astype(jnp.int32), axis=1)


def document_starts(doc_ends, positions):
    before = doc_ends[None, :] <= positions[:, None]
    return jnp.max(jnp.where(before, doc_ends[None, :], 0), axis=1)


def attention_kernel(lo_ref, hi_ref, qdf_ref, qdl_ref, kdf_ref, kdl_ref, q_ref, kt_ref, v_ref,
                     qd_ref, kd_ref, *rest, heads, causal, first, last, scaling):
    if first:
        o_refs, (m_sc, l_sc, acc_sc) = rest[:-3], rest[-3:]
    else:
        (m_in, l_in, acc_in), o_refs, (m_sc, l_sc, acc_sc) = rest[:3], rest[3:-3], rest[-3:]
    block = pl.program_id(0)
    lo = lo_ref[block]
    hi = hi_ref[block]
    q_doc_first = qdf_ref[block]
    q_single = q_doc_first == qdl_ref[block]
    lanes = acc_sc.shape[-1]
    reps = BK // lanes
    if first:
        m_sc[...] = jnp.full(m_sc.shape, -1e30, jnp.float32)
        l_sc[...] = jnp.zeros(l_sc.shape, jnp.float32)
        acc_sc[...] = jnp.zeros(acc_sc.shape, jnp.float32)
    else:
        m_sc[...] = jnp.broadcast_to(m_in[...], m_sc.shape)
        l_sc[...] = jnp.broadcast_to(l_in[...], l_sc.shape)
        acc_sc[...] = acc_in[...]

    def update(start, masked):
        keys = kt_ref[:, pl.ds(start, BK)]
        values = v_ref[pl.ds(start, BK), :]
        if masked:
            allowed = jnp.tile(qd_ref[...], (1, reps)) == kd_ref[:, pl.ds(start, BK)]
            if causal:
                rows = block * BQ + lax.broadcasted_iota(jnp.int32, (BQ, BK), 0)
                cols = start + lax.broadcasted_iota(jnp.int32, (BQ, BK), 1)
                allowed = allowed & (cols <= rows)
        for h in range(heads):
            q = q_ref[:, h * HD:(h + 1) * HD]
            s = jnp.dot(q, keys, preferred_element_type=jnp.float32) * scaling
            if masked:
                s = jnp.where(allowed, s, -1e30)
            pieces = [s[:, i * lanes:(i + 1) * lanes] for i in range(reps)]
            widest = pieces[0]
            for piece in pieces[1:]:
                widest = jnp.maximum(widest, piece)
            m_prev = m_sc[h]
            m_next = jnp.maximum(m_prev, jnp.max(widest, axis=-1, keepdims=True))
            exps = [jnp.exp2(piece - m_next) for piece in pieces]
            if masked:
                exps = [jnp.where(allowed[:, i * lanes:(i + 1) * lanes], e, 0.0)
                        for i, e in enumerate(exps)]
            total = exps[0]
            for e in exps[1:]:
                total = total + e
            fading = jnp.exp2(m_prev - m_next)
            l_sc[h] = l_sc[h] * fading + jnp.sum(total, axis=-1, keepdims=True)
            e = jnp.concatenate(exps, axis=1).astype(jnp.bfloat16)
            acc_sc[h] = acc_sc[h] * fading + jnp.dot(e, values, preferred_element_type=jnp.float32)
            m_sc[h] = m_next

    def step(j, carry):
        start = pl.multiple_of(j * BK, BK)
        k_doc_first = kdf_ref[j]
        whole = q_single & (k_doc_first == kdl_ref[j]) & (k_doc_first == q_doc_first)
        if causal:
            whole = whole & (start + BK - 1 <= block * BQ)

        @pl.when(whole)
        def _():
            update(start, False)

        @pl.when(jnp.logical_not(whole))
        def _():
            update(start, True)

        return carry

    lax.fori_loop(lo, hi, step, 0)
    if last:
        (o_ref,) = o_refs
        for h in range(heads):
            o_ref[:, h * HD:(h + 1) * HD] = (acc_sc[h] / l_sc[h]).astype(o_ref.dtype)
    else:
        m_out, l_out, acc_out = o_refs
        m_out[...] = m_sc[:, :, 0:1]
        l_out[...] = l_sc[:, :, 0:1]
        acc_out[...] = acc_sc[...]


def attend(local_q, keys_t, values, q_docs, k_docs, lo, hi, state, heads, causal, last):
    rows = local_q.shape[0]
    keys = values.shape[0]
    first = state is None
    kernel = functools.partial(attention_kernel, heads=heads, causal=causal, first=first,
                               last=last, scaling=math.log2(math.e) / math.sqrt(HD))
    per_block = lambda i, *_: (0, i, 0)
    whole = lambda i, *_: (0, 0)
    state_specs = [
        pl.BlockSpec((heads, BQ, 1), per_block),
        pl.BlockSpec((heads, BQ, 1), per_block),
        pl.BlockSpec((heads, BQ, HD), per_block),
    ]
    state_shapes = [
        jax.ShapeDtypeStruct((heads, rows, 1), jnp.float32),
        jax.ShapeDtypeStruct((heads, rows, 1), jnp.float32),
        jax.ShapeDtypeStruct((heads, rows, HD), jnp.float32),
    ]
    in_specs = [
        pl.BlockSpec((BQ, heads * HD), lambda i, *_: (i, 0)),
        pl.BlockSpec((HD, keys), whole),
        pl.BlockSpec((keys, HD), whole),
        pl.BlockSpec((BQ, HD), lambda i, *_: (i, 0)),
        pl.BlockSpec((1, keys), whole),
    ]
    operands = [
        lo, hi, q_docs[::BQ], q_docs[BQ - 1::BQ], k_docs[::BK], k_docs[BK - 1::BK],
        local_q, keys_t, values, jnp.broadcast_to(q_docs[:, None], (rows, HD)),
        k_docs.reshape(1, keys),
    ]
    if not first:
        in_specs += state_specs
        operands += list(state)
    if last:
        out_specs = pl.BlockSpec((BQ, heads * HD), lambda i, *_: (i, 0))
        out_shape = jax.ShapeDtypeStruct((rows, heads * HD), jnp.bfloat16)
    else:
        out_specs = state_specs
        out_shape = state_shapes
    grid_spec = pltpu.PrefetchScalarGridSpec(
        num_scalar_prefetch=6,
        grid=(rows // BQ,),
        in_specs=in_specs,
        out_specs=out_specs,
        scratch_shapes=[
            pltpu.VMEM((heads, BQ, HD), jnp.float32),
            pltpu.VMEM((heads, BQ, HD), jnp.float32),
            pltpu.VMEM((heads, BQ, HD), jnp.float32),
        ],
    )
    return pl.pallas_call(
        kernel,
        grid_spec=grid_spec,
        out_shape=out_shape,
        compiler_params=pltpu.CompilerParams(dimension_semantics=("arbitrary",)),
    )(*operands)


def on_device(queries, key_vectors, value_vectors, doc_lengths):
    head_dim = HD
    token_rows = queries.shape[0]
    query_total = queries.shape[1] // head_dim
    groups = lax.axis_size("hx")
    heads = query_total // groups
    message = jnp.concatenate(
        [
            key_vectors.reshape(token_rows, groups, head_dim),
            value_vectors.reshape(token_rows, groups, head_dim),
        ],
        axis=2,
    ).reshape(token_rows, -1)
    own = lax.all_to_all(message, "hx", split_axis=1, concat_axis=0, tiled=True)
    local_q = lax.all_to_all(queries, "hx", split_axis=1, concat_axis=0, tiled=True)
    chunk_rows = local_q.shape[0]
    behind = MAXDOC // chunk_rows
    per_seq = lax.axis_size("zhi")
    crossed = passed_along(own, TOKEN_AXES, 1)
    along_seq = {hop * per_seq: passed_along(own, "seq", hop) for hop in range(1, behind // per_seq + 1)}
    doc_ends = jnp.cumsum(doc_lengths).astype(jnp.int32)
    chunk = lax.axis_index("seq") * per_seq + lax.axis_index("zhi")
    chunk_first = chunk * chunk_rows
    offsets = jnp.arange(chunk_rows, dtype=jnp.int32)
    query_pos = chunk_first + offsets
    q_docs = document_ids(doc_ends, query_pos)
    doc_first = document_starts(doc_ends, query_pos[::BQ])
    lo_own = jnp.maximum(doc_first - chunk_first, 0) // BK
    hi_own = (jnp.arange(chunk_rows // BQ, dtype=jnp.int32) * BQ + BQ - 1) // BK + 1
    state = attend(local_q, own[:, :head_dim].T, own[:, head_dim:], q_docs, q_docs,
                   lo_own.astype(jnp.int32), hi_own.astype(jnp.int32), None, heads, True, False)

    def attend_chunks(parts, distances, state, last):
        kv = jnp.concatenate(parts, axis=0)
        key_pos = jnp.concatenate([chunk_first - d * chunk_rows + offsets for d in distances])
        key_docs = jnp.where(key_pos >= 0, document_ids(doc_ends, key_pos), -1)
        block_last = key_pos[BK - 1::BK]
        lo = jnp.sum((block_last[None, :] < doc_first[:, None]).astype(jnp.int32), axis=1)
        hi = jnp.full_like(lo, block_last.shape[0])
        return attend(local_q, kv[:, :head_dim].T, kv[:, head_dim:], q_docs, key_docs,
                      lo.astype(jnp.int32), hi.astype(jnp.int32), state, heads, False, last)

    far = sorted(along_seq, reverse=True)
    state = attend_chunks([along_seq[d] for d in far], far, state, False)
    crossed, state = lax.optimization_barrier((crossed, state))
    relayed = passed_along(crossed, "seq", 1)
    state = attend_chunks([crossed], [1], state, False)
    relayed, state = lax.optimization_barrier((relayed, state))
    state = attend_chunks([relayed], [per_seq + 1], state, True)
    blocks = state
    return lax.all_to_all(blocks, "hx", split_axis=0, concat_axis=1, tiled=True)


def solution(mesh):
    seq = mesh.shape["seq"]
    head = mesh.shape["head"]
    split = head // KVH
    token_mesh = Mesh(mesh.devices.reshape(seq, split, head // split), ("seq", "zhi", "hx"))
    rows = P(("seq", "zhi", "hx"), None)
    return jax.shard_map(
        on_device,
        mesh=token_mesh,
        in_specs=(rows, rows, rows, P()),
        out_specs=rows,
        check_vma=False,
    )
```

```python
import functools
import math

import jax
import jax.numpy as jnp
from jax import lax
from jax.experimental import pallas as pl
from jax.experimental.pallas import tpu as pltpu
from jax.sharding import Mesh
from jax.sharding import PartitionSpec as P

HD = 128
KVH = 8
MAXDOC = 4096
BQ = 256
BK = 512
TOKEN_AXES = ("seq", "zhi")


def passed_along(shard, axis, by):
    size = lax.axis_size(axis)
    pairs = [(i, i + by) for i in range(size) if 0 <= i + by < size]
    return lax.ppermute(shard, axis, pairs)


def document_ids(doc_ends, positions):
    return jnp.sum((doc_ends[None, :] <= positions[:, None]).astype(jnp.int32), axis=1)


def document_starts(doc_ends, positions):
    before = doc_ends[None, :] <= positions[:, None]
    return jnp.max(jnp.where(before, doc_ends[None, :], 0), axis=1)


def attention_kernel(lo_ref, hi_ref, qdf_ref, qdl_ref, kdf_ref, kdl_ref, q_ref, kt_ref, v_ref,
                     qd_ref, kd_ref, *rest, heads, causal, first, last, scaling):
    if first:
        o_refs, (m_sc, l_sc, acc_sc) = rest[:-3], rest[-3:]
    else:
        (m_in, l_in, acc_in), o_refs, (m_sc, l_sc, acc_sc) = rest[:3], rest[3:-3], rest[-3:]
    block = pl.program_id(0)
    lo = lo_ref[block]
    hi = hi_ref[block]
    q_doc_first = qdf_ref[block]
    q_single = q_doc_first == qdl_ref[block]
    lanes = acc_sc.shape[-1]
    reps = BK // lanes
    if first:
        m_sc[...] = jnp.full(m_sc.shape, -1e30, jnp.float32)
        l_sc[...] = jnp.zeros(l_sc.shape, jnp.float32)
        acc_sc[...] = jnp.zeros(acc_sc.shape, jnp.float32)
    else:
        m_sc[...] = jnp.broadcast_to(m_in[...], m_sc.shape)
        l_sc[...] = jnp.broadcast_to(l_in[...], l_sc.shape)
        acc_sc[...] = acc_in[...]

    def update(start, masked):
        keys = kt_ref[:, pl.ds(start, BK)]
        values = v_ref[pl.ds(start, BK), :]
        if masked:
            allowed = jnp.tile(qd_ref[...], (1, reps)) == kd_ref[:, pl.ds(start, BK)]
            if causal:
                rows = block * BQ + lax.broadcasted_iota(jnp.int32, (BQ, BK), 0)
                cols = start + lax.broadcasted_iota(jnp.int32, (BQ, BK), 1)
                allowed = allowed & (cols <= rows)
        for h in range(heads):
            q = q_ref[:, h * HD:(h + 1) * HD]
            s = jnp.dot(q, keys, preferred_element_type=jnp.float32) * scaling
            if masked:
                s = jnp.where(allowed, s, -1e30)
            pieces = [s[:, i * lanes:(i + 1) * lanes] for i in range(reps)]
            widest = pieces[0]
            for piece in pieces[1:]:
                widest = jnp.maximum(widest, piece)
            m_prev = m_sc[h]
            m_next = jnp.maximum(m_prev, jnp.max(widest, axis=-1, keepdims=True))
            exps = [jnp.exp2(piece - m_next) for piece in pieces]
            if masked:
                exps = [jnp.where(allowed[:, i * lanes:(i + 1) * lanes], e, 0.0)
                        for i, e in enumerate(exps)]
            total = exps[0]
            for e in exps[1:]:
                total = total + e
            fading = jnp.exp2(m_prev - m_next)
            l_sc[h] = l_sc[h] * fading + jnp.sum(total, axis=-1, keepdims=True)
            e = jnp.concatenate(exps, axis=1).astype(jnp.bfloat16)
            acc_sc[h] = acc_sc[h] * fading + jnp.dot(e, values, preferred_element_type=jnp.float32)
            m_sc[h] = m_next

    def step(j, carry):
        start = pl.multiple_of(j * BK, BK)
        k_doc_first = kdf_ref[j]
        whole = q_single & (k_doc_first == kdl_ref[j]) & (k_doc_first == q_doc_first)
        if causal:
            whole = whole & (start + BK - 1 <= block * BQ)

        @pl.when(whole)
        def _():
            update(start, False)

        @pl.when(jnp.logical_not(whole))
        def _():
            update(start, True)

        return carry

    lax.fori_loop(lo, hi, step, 0)
    if last:
        (o_ref,) = o_refs
        for h in range(heads):
            o_ref[:, h * HD:(h + 1) * HD] = (acc_sc[h] / l_sc[h]).astype(o_ref.dtype)
    else:
        m_out, l_out, acc_out = o_refs
        m_out[...] = m_sc[:, :, 0:1]
        l_out[...] = l_sc[:, :, 0:1]
        acc_out[...] = acc_sc[...]


def indices(q_docs, k_docs, lo, hi):
    rows = q_docs.shape[0]
    keys = k_docs.shape[0]
    return (lo, hi, q_docs[::BQ], q_docs[BQ - 1::BQ], k_docs[::BK], k_docs[BK - 1::BK],
            jnp.broadcast_to(q_docs[:, None], (rows, HD)), k_docs.reshape(1, keys))


def attend(local_q, keys_t, values, index, state, heads, causal, last):
    rows = local_q.shape[0]
    keys = values.shape[0]
    first = state is None
    kernel = functools.partial(attention_kernel, heads=heads, causal=causal, first=first,
                               last=last, scaling=math.log2(math.e) / math.sqrt(HD))
    per_block = lambda i, *_: (0, i, 0)
    whole = lambda i, *_: (0, 0)
    state_specs = [
        pl.BlockSpec((heads, BQ, 1), per_block),
        pl.BlockSpec((heads, BQ, 1), per_block),
        pl.BlockSpec((heads, BQ, HD), per_block),
    ]
    state_shapes = [
        jax.ShapeDtypeStruct((heads, rows, 1), jnp.float32),
        jax.ShapeDtypeStruct((heads, rows, 1), jnp.float32),
        jax.ShapeDtypeStruct((heads, rows, HD), jnp.float32),
    ]
    in_specs = [
        pl.BlockSpec((BQ, heads * HD), lambda i, *_: (i, 0)),
        pl.BlockSpec((HD, keys), whole),
        pl.BlockSpec((keys, HD), whole),
        pl.BlockSpec((BQ, HD), lambda i, *_: (i, 0)),
        pl.BlockSpec((1, keys), whole),
    ]
    lo, hi, qdf, qdl, kdf, kdl, qd_wide, kd_row = index
    operands = [lo, hi, qdf, qdl, kdf, kdl, local_q, keys_t, values, qd_wide, kd_row]
    if not first:
        in_specs += state_specs
        operands += list(state)
    if last:
        out_specs = pl.BlockSpec((BQ, heads * HD), lambda i, *_: (i, 0))
        out_shape = jax.ShapeDtypeStruct((rows, heads * HD), jnp.bfloat16)
    else:
        out_specs = state_specs
        out_shape = state_shapes
    grid_spec = pltpu.PrefetchScalarGridSpec(
        num_scalar_prefetch=6,
        grid=(rows // BQ,),
        in_specs=in_specs,
        out_specs=out_specs,
        scratch_shapes=[
            pltpu.VMEM((heads, BQ, HD), jnp.float32),
            pltpu.VMEM((heads, BQ, HD), jnp.float32),
            pltpu.VMEM((heads, BQ, HD), jnp.float32),
        ],
    )
    return pl.pallas_call(
        kernel,
        grid_spec=grid_spec,
        out_shape=out_shape,
        compiler_params=pltpu.CompilerParams(dimension_semantics=("arbitrary",)),
    )(*operands)


def on_device(queries, key_vectors, value_vectors, doc_lengths):
    head_dim = HD
    token_rows = queries.shape[0]
    query_total = queries.shape[1] // head_dim
    groups = lax.axis_size("hx")
    heads = query_total // groups
    message = jnp.concatenate(
        [
            key_vectors.reshape(token_rows, groups, head_dim),
            value_vectors.reshape(token_rows, groups, head_dim),
        ],
        axis=2,
    ).reshape(token_rows, -1)
    own = lax.all_to_all(message, "hx", split_axis=1, concat_axis=0, tiled=True)
    local_q = lax.all_to_all(queries, "hx", split_axis=1, concat_axis=0, tiled=True)
    chunk_rows = local_q.shape[0]
    behind = MAXDOC // chunk_rows
    per_seq = lax.axis_size("zhi")
    crossed = passed_along(own, TOKEN_AXES, 1)
    along_seq = {hop * per_seq: passed_along(own, "seq", hop) for hop in range(1, behind // per_seq + 1)}
    doc_ends = jnp.cumsum(doc_lengths).astype(jnp.int32)
    chunk = lax.axis_index("seq") * per_seq + lax.axis_index("zhi")
    chunk_first = chunk * chunk_rows
    offsets = jnp.arange(chunk_rows, dtype=jnp.int32)
    query_pos = chunk_first + offsets
    q_docs = document_ids(doc_ends, query_pos)
    doc_first = document_starts(doc_ends, query_pos[::BQ])
    lo_own = jnp.maximum(doc_first - chunk_first, 0) // BK
    hi_own = (jnp.arange(chunk_rows // BQ, dtype=jnp.int32) * BQ + BQ - 1) // BK + 1
    far = sorted(along_seq, reverse=True)
    plan = [far, [1], [per_seq + 1]]
    index_sets = [indices(q_docs, q_docs, lo_own.astype(jnp.int32), hi_own.astype(jnp.int32))]
    for distances in plan:
        key_pos = jnp.concatenate([chunk_first - d * chunk_rows + offsets for d in distances])
        key_docs = jnp.where(key_pos >= 0, document_ids(doc_ends, key_pos), -1)
        block_last = key_pos[BK - 1::BK]
        lo = jnp.sum((block_last[None, :] < doc_first[:, None]).astype(jnp.int32), axis=1)
        hi = jnp.full_like(lo, block_last.shape[0])
        index_sets.append(indices(q_docs, key_docs, lo.astype(jnp.int32), hi.astype(jnp.int32)))
    index_sets, local_q = lax.optimization_barrier((index_sets, local_q))
    state = attend(local_q, own[:, :head_dim].T, own[:, head_dim:], index_sets[0], None, heads,
                   True, False)

    def attend_chunks(parts, index, state, last):
        kv = jnp.concatenate(parts, axis=0)
        return attend(local_q, kv[:, :head_dim].T, kv[:, head_dim:], index, state, heads, False,
                      last)

    state = attend_chunks([along_seq[d] for d in far], index_sets[1], state, False)
    crossed, state = lax.optimization_barrier((crossed, state))
    relayed = passed_along(crossed, "seq", 1)
    state = attend_chunks([crossed], index_sets[2], state, False)
    relayed, state = lax.optimization_barrier((relayed, state))
    state = attend_chunks([relayed], index_sets[3], state, True)
    blocks = state
    return lax.all_to_all(blocks, "hx", split_axis=0, concat_axis=1, tiled=True)


def solution(mesh):
    seq = mesh.shape["seq"]
    head = mesh.shape["head"]
    split = head // KVH
    token_mesh = Mesh(mesh.devices.reshape(seq, split, head // split), ("seq", "zhi", "hx"))
    rows = P(("seq", "zhi", "hx"), None)
    return jax.shard_map(
        on_device,
        mesh=token_mesh,
        in_specs=(rows, rows, rows, P()),
        out_specs=rows,
        check_vma=False,
    )
```

```python
import functools
import math

import jax
import jax.numpy as jnp
from jax import lax
from jax.experimental import pallas as pl
from jax.experimental.pallas import tpu as pltpu
from jax.sharding import Mesh
from jax.sharding import PartitionSpec as P

HD = 128
KVH = 8
MAXDOC = 4096
BQ = 512
BK = 512
TOKEN_AXES = ("seq", "zhi")


def passed_along(shard, axis, by):
    size = lax.axis_size(axis)
    pairs = [(i, i + by) for i in range(size) if 0 <= i + by < size]
    return lax.ppermute(shard, axis, pairs)


def document_ids(doc_ends, positions):
    return jnp.sum((doc_ends[None, :] <= positions[:, None]).astype(jnp.int32), axis=1)


def document_starts(doc_ends, positions):
    before = doc_ends[None, :] <= positions[:, None]
    return jnp.max(jnp.where(before, doc_ends[None, :], 0), axis=1)


def attention_kernel(lo_ref, hi_ref, qdf_ref, qdl_ref, kdf_ref, kdl_ref, q_ref, kt_ref, v_ref,
                     qd_ref, kd_ref, *rest, heads, causal, first, last, scaling):
    if first:
        o_refs, (m_sc, l_sc, acc_sc) = rest[:-3], rest[-3:]
    else:
        (m_in, l_in, acc_in), o_refs, (m_sc, l_sc, acc_sc) = rest[:3], rest[3:-3], rest[-3:]
    block = pl.program_id(0)
    lo = lo_ref[block]
    hi = hi_ref[block]
    q_doc_first = qdf_ref[block]
    q_single = q_doc_first == qdl_ref[block]
    lanes = acc_sc.shape[-1]
    reps = BK // lanes
    if first:
        m_sc[...] = jnp.full(m_sc.shape, -1e30, jnp.float32)
        l_sc[...] = jnp.zeros(l_sc.shape, jnp.float32)
        acc_sc[...] = jnp.zeros(acc_sc.shape, jnp.float32)
    else:
        m_sc[...] = jnp.broadcast_to(m_in[...], m_sc.shape)
        l_sc[...] = jnp.broadcast_to(l_in[...], l_sc.shape)
        acc_sc[...] = acc_in[...]

    def update(start, masked):
        keys = kt_ref[:, pl.ds(start, BK)]
        values = v_ref[pl.ds(start, BK), :]
        if masked:
            allowed = jnp.tile(qd_ref[...], (1, reps)) == kd_ref[:, pl.ds(start, BK)]
            if causal:
                rows = block * BQ + lax.broadcasted_iota(jnp.int32, (BQ, BK), 0)
                cols = start + lax.broadcasted_iota(jnp.int32, (BQ, BK), 1)
                allowed = allowed & (cols <= rows)
        for h in range(heads):
            q = q_ref[:, h * HD:(h + 1) * HD]
            s = jnp.dot(q, keys, preferred_element_type=jnp.float32) * scaling
            if masked:
                s = jnp.where(allowed, s, -1e30)
            pieces = [s[:, i * lanes:(i + 1) * lanes] for i in range(reps)]
            widest = pieces[0]
            for piece in pieces[1:]:
                widest = jnp.maximum(widest, piece)
            m_prev = m_sc[h]
            m_next = jnp.maximum(m_prev, jnp.max(widest, axis=-1, keepdims=True))
            exps = [jnp.exp2(piece - m_next) for piece in pieces]
            if masked:
                exps = [jnp.where(allowed[:, i * lanes:(i + 1) * lanes], e, 0.0)
                        for i, e in enumerate(exps)]
            total = exps[0]
            for e in exps[1:]:
                total = total + e
            fading = jnp.exp2(m_prev - m_next)
            l_sc[h] = l_sc[h] * fading + jnp.sum(total, axis=-1, keepdims=True)
            e = jnp.concatenate(exps, axis=1).astype(jnp.bfloat16)
            acc_sc[h] = acc_sc[h] * fading + jnp.dot(e, values, preferred_element_type=jnp.float32)
            m_sc[h] = m_next

    def step(j, carry):
        start = pl.multiple_of(j * BK, BK)
        k_doc_first = kdf_ref[j]
        whole = q_single & (k_doc_first == kdl_ref[j]) & (k_doc_first == q_doc_first)
        if causal:
            whole = whole & (start + BK - 1 <= block * BQ)

        @pl.when(whole)
        def _():
            update(start, False)

        @pl.when(jnp.logical_not(whole))
        def _():
            update(start, True)

        return carry

    lax.fori_loop(lo, hi, step, 0)
    if last:
        (o_ref,) = o_refs
        for h in range(heads):
            o_ref[:, h * HD:(h + 1) * HD] = (acc_sc[h] / l_sc[h]).astype(o_ref.dtype)
    else:
        m_out, l_out, acc_out = o_refs
        m_out[...] = m_sc[:, :, 0:1]
        l_out[...] = l_sc[:, :, 0:1]
        acc_out[...] = acc_sc[...]


def indices(q_docs, k_docs, lo, hi):
    rows = q_docs.shape[0]
    keys = k_docs.shape[0]
    return (lo, hi, q_docs[::BQ], q_docs[BQ - 1::BQ], k_docs[::BK], k_docs[BK - 1::BK],
            jnp.broadcast_to(q_docs[:, None], (rows, HD)), k_docs.reshape(1, keys))


def attend(local_q, keys_t, values, index, state, heads, causal, last):
    rows = local_q.shape[0]
    keys = values.shape[0]
    first = state is None
    kernel = functools.partial(attention_kernel, heads=heads, causal=causal, first=first,
                               last=last, scaling=math.log2(math.e) / math.sqrt(HD))
    per_block = lambda i, *_: (0, i, 0)
    whole = lambda i, *_: (0, 0)
    state_specs = [
        pl.BlockSpec((heads, BQ, 1), per_block),
        pl.BlockSpec((heads, BQ, 1), per_block),
        pl.BlockSpec((heads, BQ, HD), per_block),
    ]
    state_shapes = [
        jax.ShapeDtypeStruct((heads, rows, 1), jnp.float32),
        jax.ShapeDtypeStruct((heads, rows, 1), jnp.float32),
        jax.ShapeDtypeStruct((heads, rows, HD), jnp.float32),
    ]
    in_specs = [
        pl.BlockSpec((BQ, heads * HD), lambda i, *_: (i, 0)),
        pl.BlockSpec((HD, keys), whole),
        pl.BlockSpec((keys, HD), whole),
        pl.BlockSpec((BQ, HD), lambda i, *_: (i, 0)),
        pl.BlockSpec((1, keys), whole),
    ]
    lo, hi, qdf, qdl, kdf, kdl, qd_wide, kd_row = index
    operands = [lo, hi, qdf, qdl, kdf, kdl, local_q, keys_t, values, qd_wide, kd_row]
    if not first:
        in_specs += state_specs
        operands += list(state)
    if last:
        out_specs = pl.BlockSpec((BQ, heads * HD), lambda i, *_: (i, 0))
        out_shape = jax.ShapeDtypeStruct((rows, heads * HD), jnp.bfloat16)
    else:
        out_specs = state_specs
        out_shape = state_shapes
    grid_spec = pltpu.PrefetchScalarGridSpec(
        num_scalar_prefetch=6,
        grid=(rows // BQ,),
        in_specs=in_specs,
        out_specs=out_specs,
        scratch_shapes=[
            pltpu.VMEM((heads, BQ, HD), jnp.float32),
            pltpu.VMEM((heads, BQ, HD), jnp.float32),
            pltpu.VMEM((heads, BQ, HD), jnp.float32),
        ],
    )
    return pl.pallas_call(
        kernel,
        grid_spec=grid_spec,
        out_shape=out_shape,
        compiler_params=pltpu.CompilerParams(dimension_semantics=("arbitrary",)),
    )(*operands)


def on_device(queries, key_vectors, value_vectors, doc_lengths):
    head_dim = HD
    token_rows = queries.shape[0]
    query_total = queries.shape[1] // head_dim
    groups = lax.axis_size("hx")
    heads = query_total // groups
    message = jnp.concatenate(
        [
            key_vectors.reshape(token_rows, groups, head_dim),
            value_vectors.reshape(token_rows, groups, head_dim),
        ],
        axis=2,
    ).reshape(token_rows, -1)
    own = lax.all_to_all(message, "hx", split_axis=1, concat_axis=0, tiled=True)
    local_q = lax.all_to_all(queries, "hx", split_axis=1, concat_axis=0, tiled=True)
    chunk_rows = local_q.shape[0]
    behind = MAXDOC // chunk_rows
    per_seq = lax.axis_size("zhi")
    crossed = passed_along(own, TOKEN_AXES, 1)
    along_seq = {hop * per_seq: passed_along(own, "seq", hop) for hop in range(1, behind // per_seq + 1)}
    doc_ends = jnp.cumsum(doc_lengths).astype(jnp.int32)
    chunk = lax.axis_index("seq") * per_seq + lax.axis_index("zhi")
    chunk_first = chunk * chunk_rows
    offsets = jnp.arange(chunk_rows, dtype=jnp.int32)
    query_pos = chunk_first + offsets
    q_docs = document_ids(doc_ends, query_pos)
    doc_first = document_starts(doc_ends, query_pos[::BQ])
    lo_own = jnp.maximum(doc_first - chunk_first, 0) // BK
    hi_own = (jnp.arange(chunk_rows // BQ, dtype=jnp.int32) * BQ + BQ - 1) // BK + 1
    far = sorted(along_seq, reverse=True)
    plan = [far, [1], [per_seq + 1]]
    index_sets = [indices(q_docs, q_docs, lo_own.astype(jnp.int32), hi_own.astype(jnp.int32))]
    for distances in plan:
        key_pos = jnp.concatenate([chunk_first - d * chunk_rows + offsets for d in distances])
        key_docs = jnp.where(key_pos >= 0, document_ids(doc_ends, key_pos), -1)
        block_last = key_pos[BK - 1::BK]
        lo = jnp.sum((block_last[None, :] < doc_first[:, None]).astype(jnp.int32), axis=1)
        hi = jnp.full_like(lo, block_last.shape[0])
        index_sets.append(indices(q_docs, key_docs, lo.astype(jnp.int32), hi.astype(jnp.int32)))
    index_sets, local_q = lax.optimization_barrier((index_sets, local_q))
    state = attend(local_q, own[:, :head_dim].T, own[:, head_dim:], index_sets[0], None, heads,
                   True, False)

    def attend_chunks(parts, index, state, last):
        kv = jnp.concatenate(parts, axis=0)
        return attend(local_q, kv[:, :head_dim].T, kv[:, head_dim:], index, state, heads, False,
                      last)

    state = attend_chunks([along_seq[d] for d in far], index_sets[1], state, False)
    crossed, state = lax.optimization_barrier((crossed, state))
    relayed = passed_along(crossed, "seq", 1)
    state = attend_chunks([crossed], index_sets[2], state, False)
    relayed, state = lax.optimization_barrier((relayed, state))
    state = attend_chunks([relayed], index_sets[3], state, True)
    blocks = state
    return lax.all_to_all(blocks, "hx", split_axis=0, concat_axis=1, tiled=True)


def solution(mesh):
    seq = mesh.shape["seq"]
    head = mesh.shape["head"]
    split = head // KVH
    token_mesh = Mesh(mesh.devices.reshape(seq, split, head // split), ("seq", "zhi", "hx"))
    rows = P(("seq", "zhi", "hx"), None)
    return jax.shard_map(
        on_device,
        mesh=token_mesh,
        in_specs=(rows, rows, rows, P()),
        out_specs=rows,
        check_vma=False,
    )
```
